512 devices in a mesh: pipe: 4 (over y_hi, core), ctx: 16 (over z), dp: 8 (over y_lo, x).
Axes of the slice: x: 4, y: 4 (y_hi: 2, y_lo: 2; y = y_hi * 2 + y_lo), z: 16, core: 2. Of those that a mesh axis runs over, the one named last changes fastest.
Arguments:
- clean_latent: float32 [2, 8, 1024, 64], P(None, 'dp', 'ctx'), may hold values from -6 to 6
- noise_latent: float32 [2, 8, 1024, 64], P(None, 'dp', 'ctx'), may hold values from -6 to 6
- time_index: int32 [2, 8], P(None, 'dp'), may hold values from 0 to 999
- frame_ids: int32 [2, 8, 1024], P(None, 'dp'), may hold values from 0 to 15, never falling along the last dimension, each value on 1 to 128 neighbouring positions
- embed_weight: bfloat16 [64, 1536], replicated, may hold values from -0.75 to 0.75
- time_vector: float32 [1536], replicated, may hold values from -5 to 5
- query_weight: bfloat16 [4, 1536, 1536], P('pipe', 'dp'), may hold values from -1 to 41
- key_weight: bfloat16 [4, 1536, 1536], P('pipe', 'dp'), may hold values from -1 to 3
- norm_gain: float32 [4, 1536], P('pipe'), may hold values from 0.1 to 1.9
- head_gain: float32 [1536], replicated, may hold values from 0.1 to 1.9
- head_weight: bfloat16 [1536, 64], P(None, 'pipe'), may hold values from -0.15625 to 0.15625
Outputs:
- velocity: float32 [2, 8, 1024, 64], P(None, 'dp', 'ctx', 'pipe')
- head_grad: float32 [1536, 64], P('dp', 'pipe')
The draws below stay inside these ranges and needn't reach their ends.
Inputs may be any that keep to these rules, and one draw needn't show every extreme that they name: `frame_ids`: along each sequence the frame number never falls and starts at 0; each frame holds 1 to 128 patches, and some frame holds exactly 128.
All inputs are finite; a program needn't handle non-finite values.
Results may differ from the reference program's by a relative error of at most 0.014.
The reference program's roundings to bfloat16 on the way count: a program that leaves them out, or rounds other values in their place, can miss the bound.
Values may be sent and summed in bfloat16 or wider, within the bound.
No kernel may reach another device: no remote copies, remote signals or barrier semaphores. Data moves between devices by JAX's collectives and lax.ppermute only.
A program may use at most 128 MiB of HBM per device.

```python
import math
import jax
import jax.numpy as jnp
import numpy as np
from jax import lax

HEADS = 16
HEAD = 96
D = 1536
P_SIZE = 64
MB = 2
SECTIONS = 4
SAMPLES = 8
SEQ = 1024
BLOCK = 128
FRAMES = 16


def draw_query_weight(key, part):
    base_key, scale_key = jax.random.split(jax.random.fold_in(key, 17))
    base = jax.random.normal(base_key, (SECTIONS, D, D), jnp.float32) * D ** (-0.5)
    identity = (jnp.arange(D)[:, None] == jnp.arange(D)[None, :]).astype(jnp.float32)
    strength = jax.random.uniform(scale_key, (SECTIONS, 1, HEADS), jnp.float32, 0.3, 0.8)
    column_scale = jnp.repeat(strength, HEAD, axis=2)
    return (base + identity[None] * column_scale).astype(jnp.bfloat16)


def draw_key_weight(key, part):
    base_key, scale_key = jax.random.split(jax.random.fold_in(key, 29))
    base = jax.random.normal(base_key, (SECTIONS, D, D), jnp.float32) * D ** (-0.5)
    identity = (jnp.arange(D)[:, None] == jnp.arange(D)[None, :]).astype(jnp.float32)
    strength = jax.random.uniform(scale_key, (SECTIONS, 1, HEADS), jnp.float32, 0.3, 0.8)
    column_scale = jnp.repeat(strength, HEAD, axis=2)
    return (base + identity[None] * column_scale).astype(jnp.bfloat16)


def touch_ends(values, stream_key, least, top_value):
    longest = values.shape.index(max(values.shape))
    spots = []
    for shift in (0, 1):
        where = [jax.random.randint(jax.random.fold_in(stream_key, axis), (), 0, length) for axis, length in enumerate(values.shape)]
        where[longest] = (where[longest] + shift) % values.shape[longest]
        spots.append(tuple(where))
    return values.at[spots[0]].set(least).at[spots[1]].set(top_value)


def levels(rng, shape, cuts, smallest, largest):
    def one(dim, shards_of):
        heights = jax.random.uniform(jax.random.fold_in(jax.random.fold_in(rng, 6), dim), (shards_of,), jnp.float32, smallest / len(cuts), largest / len(cuts))
        return jnp.repeat(jnp.exp(heights), shape[dim] // shards_of).reshape((-1,) + (1,) * (len(shape) - dim - 1))

    factor_of = one(*cuts[0])
    for cut in cuts[1:]:
        factor_of = factor_of * one(*cut)
    return factor_of


def split_up(amount, total, limit, slope):
    weights = [(1 << 20) // math.isqrt(rank ** slope) + 1 for rank in range(2, amount + 1)]
    surplus, counts = total - limit - (amount - 1), [1] * (amount - 1)
    while surplus > 0:
        movable = [i for i in range(amount - 1) if counts[i] < limit]
        mass, remaining = sum([weights[i] for i in movable]), surplus
        for i in movable:
            extra = min(limit - counts[i], max(1, remaining * weights[i] // mass), surplus)
            counts[i] = counts[i] + extra
            surplus = surplus - extra
    return np.array([limit] + counts)


def ragged_sizes(own_key, number_of, total, bound, skew):
    if number_of == 2:
        one = jax.random.randint(own_key, (), max(1, total - bound), min(bound, total - 1) + 1)
        return jnp.stack([one, total - one])
    tallies = jnp.asarray(split_up(number_of, total, bound, skew), jnp.int32)
    couples = (number_of - 1) // 2
    giver, taker = tallies[1:1 + 2 * couples:2], tallies[2:2 + 2 * couples:2]
    slack = jnp.minimum(giver - 1, bound - taker)
    shifted = jax.random.randint(jax.random.fold_in(own_key, 1), (couples,), 0, 1 << 20) % (slack + 1)
    tallies = tallies.at[1:1 + 2 * couples:2].set(giver - shifted).at[2:2 + 2 * couples:2].set(taker + shifted)
    return tallies[jax.random.permutation(jax.random.fold_in(own_key, 2), number_of)]


def centred(stream_key, extent, width, reach, pieces=(), kind=jnp.bfloat16):
    loudness = levels(stream_key, extent, pieces, -0.22, 0.18) if pieces else 1.0
    entries = jax.random.normal(stream_key, extent, jnp.float32) * width * loudness
    return jnp.minimum(jnp.maximum(entries, -reach), reach).astype(kind)


def setup_inputs(seed: int = 0) -> dict:
    seeds = jax.random.split(jax.random.key(seed), 12)
    return {
        "clean_latent": centred(seeds[0], (MB, SAMPLES, SEQ, P_SIZE), 1.0, 6.0, ((1, 8), (2, 16)), jnp.float32),
        "noise_latent": centred(seeds[1], (MB, SAMPLES, SEQ, P_SIZE), 1.0, 6.0, ((1, 8), (2, 16)), jnp.float32),
        "time_index": touch_ends(jax.random.randint(seeds[2], (MB, SAMPLES), 0, 1000), jax.random.fold_in(seeds[2], 1), 0, 999).astype(jnp.int32),
        "frame_ids": jax.vmap(lambda own: jnp.searchsorted(jnp.cumsum(ragged_sizes(own, FRAMES, SEQ, BLOCK, 2)), jnp.arange(SEQ), side="right"))(jax.random.split(seeds[3], MB * SAMPLES)).reshape((MB, SAMPLES, SEQ)).astype(jnp.int32),
        "embed_weight": centred(seeds[4], (P_SIZE, D), P_SIZE ** -0.5, 0.75),
        "time_vector": centred(seeds[5], (D,), 1.0, 5.0, (), jnp.float32),
        "query_weight": draw_query_weight(jax.random.fold_in(seeds[11], 71), 0),
        "key_weight": draw_key_weight(jax.random.fold_in(seeds[11], 71), 0),
        "norm_gain": jnp.clip(1.0 + 0.18 * jax.random.normal(seeds[8], (SECTIONS, D), jnp.float32), 0.1, 1.9),
        "head_gain": jnp.clip(1.0 + 0.18 * jax.random.normal(seeds[9], (D,), jnp.float32), 0.1, 1.9),
        "head_weight": centred(seeds[10], (D, P_SIZE), D ** -0.5, 0.15625, ((1, 4),)),
    }


epsilon = 1e-06

def rms_scale(values, gain_row):
    return values * lax.rsqrt(lax.optimization_barrier(jnp.mean(values * values, axis=-1, keepdims=True)) + epsilon) * gain_row

def attend(normed, queries, keys, frame_row):
    query_heads = queries.reshape(SEQ, HEADS, HEAD).astype(jnp.float32)
    key_heads = keys.reshape(SEQ, HEADS, HEAD).astype(jnp.float32)
    value_heads = normed.reshape(SEQ, HEADS, HEAD).astype(jnp.float32)
    scores = jnp.einsum('shd,khd->hsk', query_heads, key_heads) * HEAD ** (-0.5)
    allowed = frame_row[None, :] <= frame_row[:, None]
    scores = jnp.where(allowed[None], scores, -1e+30)
    row_max = lax.optimization_barrier(jnp.max(scores, axis=-1, keepdims=True))
    weights = jnp.where(allowed[None], jnp.exp(scores - row_max), 0.0)
    row_sum = lax.optimization_barrier(jnp.sum(weights, axis=-1))
    rounded = lax.optimization_barrier(weights.astype(jnp.bfloat16)).astype(jnp.float32)
    mixed = jnp.einsum('hsk,khd->hsd', rounded, value_heads) / row_sum[..., None]
    return mixed.transpose(1, 0, 2).reshape(SEQ, D).astype(jnp.bfloat16)

def section(state, gain_row, weight, key_mat, frame_row):
    wide_state = state.astype(jnp.float32)
    normed = rms_scale(wide_state, gain_row).astype(jnp.bfloat16)
    queries = jnp.dot(normed, weight, preferred_element_type=jnp.float32).astype(jnp.bfloat16)
    keys = jnp.dot(normed, key_mat, preferred_element_type=jnp.float32).astype(jnp.bfloat16)
    mixed = attend(normed, queries, keys, frame_row)
    return (wide_state + mixed.astype(jnp.float32)).astype(jnp.bfloat16)

def reference(clean_latent, noise_latent, time_index, frame_ids, embed_weight, time_vector, query_weight, key_weight, norm_gain, head_gain, head_weight):
    flow_time = ((time_index.astype(jnp.float32) + 0.5) / 1000.0)[:, :, None, None]
    noisy_input = ((1.0 - flow_time) * noise_latent + flow_time * clean_latent).astype(jnp.bfloat16)
    target = clean_latent - noise_latent
    state = jnp.einsum('mbsp,pd->mbsd', noisy_input.astype(jnp.float32), embed_weight.astype(jnp.float32))
    state = (state + flow_time * time_vector).astype(jnp.bfloat16)
    flat_state = state.reshape(MB * SAMPLES, SEQ, D)
    flat_frames = frame_ids.reshape(MB * SAMPLES, SEQ)
    for section_index in range(SECTIONS):

        def one_sequence(packed, section_index=section_index):
            return section(packed[0], norm_gain[section_index], query_weight[section_index], key_weight[section_index], packed[1])
        flat_state = lax.map(one_sequence, (flat_state, flat_frames))
    final_norm = rms_scale(flat_state.astype(jnp.float32), head_gain).astype(jnp.bfloat16).reshape(-1, D)
    velocity_flat = jnp.dot(final_norm, head_weight, preferred_element_type=jnp.float32)
    velocity = velocity_flat.reshape(MB, SAMPLES, SEQ, P_SIZE)
    residue = velocity_flat - target.reshape(-1, P_SIZE)
    head_grad = jnp.dot(final_norm.astype(jnp.float32).T, residue, precision=lax.Precision.HIGHEST) / SEQ
    return (velocity, head_grad)
```

```python
import jax
import jax.numpy as jnp
from jax import lax
from jax.sharding import PartitionSpec as P

HEAD = 96


epsilon = 1e-06


def shifted(value, axis, steps):
    count = lax.axis_size(axis)
    first, last = (max(0, -steps), min(count, count - steps))
    return lax.ppermute(value, axis, [(source, source + steps) for source in range(first, last)])


def broadcast(value, axis, source):
    kept = jnp.where(lax.axis_index(axis) == source, value, 0).astype(value.dtype)
    return lax.psum(kept, axis)


def rms_scale(values, gain_row):
    return (
        values * lax.rsqrt(jnp.mean(values * values, axis=-1, keepdims=True) + epsilon) * gain_row
    )


def on_device(
    clean_latent,
    noise_latent,
    time_index,
    frame_ids,
    embed_weight,
    time_vector,
    query_weight,
    key_weight,
    norm_gain,
    head_gain,
    head_weight,
):
    phase_index = lax.axis_index("pipe")
    phase_count = lax.axis_size("pipe")
    cycle_size = lax.axis_size("ctx")
    micro_count = clean_latent.shape[0]
    local_rows = clean_latent.shape[2]
    model_width = embed_weight.shape[1]
    head_count = model_width // HEAD
    local_heads = head_count // cycle_size
    local_width = local_heads * HEAD
    seq_total = local_rows * cycle_size
    score_scale = HEAD ** (-0.5)
    flow_time = ((time_index.astype(jnp.float32) + 0.5) / 1000.0)[:, :, None, None]
    noisy_input = ((1.0 - flow_time) * noise_latent + flow_time * clean_latent).astype(jnp.bfloat16)
    target = clean_latent - noise_latent
    embedded = jnp.einsum(
        "mbsp,pd->mbsd", noisy_input, embed_weight, preferred_element_type=jnp.float32
    )
    embedded = (embedded + flow_time * time_vector).astype(jnp.bfloat16)
    gathered = (
        lax.all_gather(query_weight, "dp", axis=1, tiled=True),
        lax.all_gather(key_weight, "dp", axis=1, tiled=True),
    )
    head_full = lax.all_gather(head_weight, "pipe", axis=1, tiled=True)
    full_query = gathered[0][0]
    full_key = gathered[1][0]
    section_gain = norm_gain[0]

    def attention(by_heads, frame_row):
        query_all = by_heads[0].reshape(seq_total, local_heads, HEAD)
        key_all = by_heads[1].reshape(seq_total, local_heads, HEAD)
        value_all = by_heads[2].reshape(seq_total, local_heads, HEAD)
        allowed = frame_row[None, :] <= frame_row[:, None]
        scores = (
            jnp.einsum("shd,khd->hsk", query_all, key_all, preferred_element_type=jnp.float32)
            * score_scale
        )
        scores = jnp.where(allowed[None], scores, -1e30)
        row_max = jnp.max(scores, axis=-1, keepdims=True)
        weights = jnp.where(allowed[None], jnp.exp(scores - row_max), 0.0)
        row_sum = jnp.sum(weights, axis=-1)
        mixed = jnp.einsum(
            "hsk,khd->hsd",
            weights.astype(jnp.bfloat16),
            value_all,
            preferred_element_type=jnp.float32,
        ) / row_sum[..., None]
        return mixed.transpose(1, 0, 2).reshape(seq_total, local_width).astype(jnp.bfloat16)

    incoming = jnp.zeros((1, local_rows, model_width), jnp.bfloat16)
    finals = []
    moment_count = micro_count + phase_count - 1
    for moment in range(moment_count):
        micro_slot = jnp.clip(moment - phase_index, 0, micro_count - 1)
        active = jnp.logical_and(moment >= phase_index, moment - phase_index < micro_count)
        current = jnp.where(phase_index == 0, embedded[min(moment, micro_count - 1)], incoming)
        frame_row = lax.dynamic_index_in_dim(frame_ids, micro_slot, 0, keepdims=False)[0]
        wide_state = current.astype(jnp.float32)
        normed = rms_scale(wide_state, section_gain).astype(jnp.bfloat16)[0]

        def project(source):
            queries = jnp.dot(source, full_query, preferred_element_type=jnp.float32).astype(
                jnp.bfloat16
            )
            keys = jnp.dot(source, full_key, preferred_element_type=jnp.float32).astype(
                jnp.bfloat16
            )
            return jnp.stack((queries, keys, source), axis=0)

        def blank_triple(source):
            return jnp.zeros((3,) + source.shape, jnp.bfloat16)

        triple = lax.cond(active, project, blank_triple, normed)
        section_by_heads = lax.all_to_all(triple, "ctx", split_axis=2, concat_axis=1, tiled=True)

        def run_attention(arrived):
            return attention(arrived, frame_row)

        def blank_heads(arrived):
            return jnp.zeros((seq_total, local_width), jnp.bfloat16)

        mixed_heads = lax.cond(active, run_attention, blank_heads, section_by_heads)
        mixed = lax.all_to_all(mixed_heads, "ctx", split_axis=0, concat_axis=1, tiled=True)
        result = (wide_state + mixed.astype(jnp.float32)[None]).astype(jnp.bfloat16)
        if moment + 1 < moment_count:
            incoming = shifted(result, "pipe", 1)
        if moment >= phase_count - 1:
            finals.append(result)
    final_state = jnp.stack(finals, axis=0)
    last_phase = phase_count - 1
    is_last = phase_index == last_phase
    head_cols = head_weight.shape[1]
    final_norm = rms_scale(final_state.astype(jnp.float32), head_gain).astype(jnp.bfloat16)
    velocity_all = jnp.einsum(
        "mbsd,dp->mbsp", final_norm, head_full, preferred_element_type=jnp.float32
    )
    residue = velocity_all - target
    grad_all = jnp.einsum(
        "mbsd,mbsp->dp", final_norm.astype(jnp.float32), residue, precision=lax.Precision.HIGHEST
    ) / float(seq_total)
    arrived = jnp.zeros(velocity_all.shape[:3] + (head_cols,), jnp.float32)
    for target_phase in range(last_phase):
        piece = velocity_all[..., target_phase * head_cols : (target_phase + 1) * head_cols]
        arrived = arrived + lax.ppermute(piece, "pipe", [(last_phase, target_phase)])
    own_piece = velocity_all[..., last_phase * head_cols :]
    velocity = jnp.where(is_last, own_piece, arrived)
    dp_count = lax.axis_size("dp")
    grad_rows = model_width // dp_count
    kept = jnp.where(is_last, grad_all, 0.0)
    blocks = (
        kept.reshape(dp_count, grad_rows, phase_count, head_cols)
        .transpose(0, 2, 1, 3)
        .reshape(dp_count * phase_count, grad_rows, head_cols)
    )
    scattered = lax.psum_scatter(blocks, ("dp", "pipe"), scatter_dimension=0, tiled=True)
    gradient = lax.psum(scattered.reshape(grad_rows, head_cols), "ctx")
    return (velocity, gradient)


def solution(mesh):
    placed = (
        P(None, "dp", "ctx", None),
        P(None, "dp", "ctx", None),
        P(None, "dp"),
        P(None, "dp", None),
        P(),
        P(),
        P("pipe", "dp", None),
        P("pipe", "dp", None),
        P("pipe", None),
        P(),
        P(None, "pipe"),
    )
    return jax.shard_map(
        on_device,
        mesh=mesh,
        in_specs=placed,
        out_specs=(P(None, "dp", "ctx", "pipe"), P("dp", "pipe")),
        check_vma=False,
    )
```

```python
import jax
import jax.numpy as jnp
from jax import lax
from jax.sharding import PartitionSpec as P

HEAD = 96


epsilon = 1e-06


def shifted(value, axis, steps):
    count = lax.axis_size(axis)
    first, last = (max(0, -steps), min(count, count - steps))
    return lax.ppermute(value, axis, [(source, source + steps) for source in range(first, last)])


def rms_scale(values, gain_row):
    return (
        values * lax.rsqrt(jnp.mean(values * values, axis=-1, keepdims=True) + epsilon) * gain_row
    )


def on_device(
    clean_latent,
    noise_latent,
    time_index,
    frame_ids,
    embed_weight,
    time_vector,
    query_weight,
    key_weight,
    norm_gain,
    head_gain,
    head_weight,
):
    phase_index = lax.axis_index("pipe")
    phase_count = lax.axis_size("pipe")
    cycle_index = lax.axis_index("ctx")
    cycle_size = lax.axis_size("ctx")
    dp_count = lax.axis_size("dp")
    micro_count = clean_latent.shape[0]
    local_rows = clean_latent.shape[2]
    model_width = embed_weight.shape[1]
    head_count = model_width // HEAD
    local_heads = head_count // cycle_size
    local_width = local_heads * HEAD
    seq_total = local_rows * cycle_size
    score_scale = HEAD ** (-0.5)
    flow_time = ((time_index.astype(jnp.float32) + 0.5) / 1000.0)[:, :, None, None]
    noisy_input = ((1.0 - flow_time) * noise_latent + flow_time * clean_latent).astype(jnp.bfloat16)
    target = clean_latent - noise_latent
    embedded = jnp.einsum(
        "mbsp,pd->mbsd", noisy_input, embed_weight, preferred_element_type=jnp.float32
    )
    embedded = (embedded + flow_time * time_vector).astype(jnp.bfloat16)
    column_start = cycle_index * local_width
    query_cols = lax.dynamic_slice_in_dim(query_weight[0], column_start, local_width, 1)
    key_cols = lax.dynamic_slice_in_dim(key_weight[0], column_start, local_width, 1)
    head_query = lax.all_gather(query_cols, "dp", axis=0, tiled=True)
    head_key = lax.all_gather(key_cols, "dp", axis=0, tiled=True)
    head_full = lax.all_gather(head_weight, "pipe", axis=1, tiled=True)
    section_gain = norm_gain[0]

    def attention(query_all, key_all, value_all, frame_row):
        query_all = query_all.reshape(seq_total, local_heads, HEAD)
        key_all = key_all.reshape(seq_total, local_heads, HEAD)
        value_all = value_all.reshape(seq_total, local_heads, HEAD)
        allowed = frame_row[None, :] <= frame_row[:, None]
        scores = (
            jnp.einsum("shd,khd->hsk", query_all, key_all, preferred_element_type=jnp.float32)
            * score_scale
        )
        scores = jnp.where(allowed[None], scores, -1e30)
        row_max = jnp.max(scores, axis=-1, keepdims=True)
        weights = jnp.where(allowed[None], jnp.exp(scores - row_max), 0.0)
        row_sum = jnp.sum(weights, axis=-1)
        mixed = jnp.einsum(
            "hsk,khd->hsd",
            weights.astype(jnp.bfloat16),
            value_all,
            preferred_element_type=jnp.float32,
        ) / row_sum[..., None]
        return mixed.transpose(1, 0, 2).reshape(seq_total, local_width).astype(jnp.bfloat16)

    def mix_heads(rows_all, frame_row):
        queries = jnp.dot(rows_all, head_query, preferred_element_type=jnp.float32).astype(
            jnp.bfloat16
        )
        keys = jnp.dot(rows_all, head_key, preferred_element_type=jnp.float32).astype(
            jnp.bfloat16
        )
        values = lax.dynamic_slice_in_dim(rows_all, column_start, local_width, 1)
        return attention(queries, keys, values, frame_row)

    def blank_heads(rows_all, frame_row):
        return jnp.zeros((seq_total, local_width), jnp.bfloat16)

    incoming = jnp.zeros((1, local_rows, model_width), jnp.bfloat16)
    finals = []
    moment_count = micro_count + phase_count - 1
    for moment in range(moment_count):
        micro_slot = jnp.clip(moment - phase_index, 0, micro_count - 1)
        active = jnp.logical_and(moment >= phase_index, moment - phase_index < micro_count)
        current = jnp.where(phase_index == 0, embedded[min(moment, micro_count - 1)], incoming)
        frame_row = lax.dynamic_index_in_dim(frame_ids, micro_slot, 0, keepdims=False)[0]
        wide_state = current.astype(jnp.float32)
        normed = rms_scale(wide_state, section_gain).astype(jnp.bfloat16)[0]
        rows_all = lax.all_gather(normed, "ctx", axis=0, tiled=True)
        mixed_heads = lax.cond(active, mix_heads, blank_heads, rows_all, frame_row)
        mixed = lax.all_to_all(mixed_heads, "ctx", split_axis=0, concat_axis=1, tiled=True)
        result = (wide_state + mixed.astype(jnp.float32)[None]).astype(jnp.bfloat16)
        if moment + 1 < moment_count:
            incoming = shifted(result, "pipe", 1)
        if moment >= phase_count - 1:
            finals.append(result)
    final_state = jnp.stack(finals, axis=0)
    last_phase = phase_count - 1
    is_last = phase_index == last_phase
    head_cols = head_weight.shape[1]
    final_norm = rms_scale(final_state.astype(jnp.float32), head_gain).astype(jnp.bfloat16)
    velocity_all = jnp.einsum(
        "mbsd,dp->mbsp", final_norm, head_full, preferred_element_type=jnp.float32
    )
    residue = velocity_all - target
    grad_all = jnp.einsum(
        "mbsd,mbsp->dp", final_norm.astype(jnp.float32), residue, precision=lax.Precision.HIGHEST
    ) / float(seq_total)
    grad_rows = lax.psum_scatter(grad_all, "dp", scatter_dimension=0, tiled=True)
    grad_rows = lax.psum(grad_rows, "ctx")
    velocity_in = jnp.zeros(velocity_all.shape[:3] + (head_cols,), jnp.float32)
    gradient_in = jnp.zeros((grad_rows.shape[0], head_cols), jnp.float32)
    for target_phase in range(last_phase):
        cols = slice(target_phase * head_cols, (target_phase + 1) * head_cols)
        pair = [(last_phase, target_phase)]
        velocity_in = velocity_in + lax.ppermute(velocity_all[..., cols], "pipe", pair)
        gradient_in = gradient_in + lax.ppermute(grad_rows[:, cols], "pipe", pair)
    own_cols = slice(last_phase * head_cols, phase_count * head_cols)
    velocity = jnp.where(is_last, velocity_all[..., own_cols], velocity_in)
    gradient = jnp.where(is_last, grad_rows[:, own_cols], gradient_in)
    return (velocity, gradient)


def solution(mesh):
    placed = (
        P(None, "dp", "ctx", None),
        P(None, "dp", "ctx", None),
        P(None, "dp"),
        P(None, "dp", None),
        P(),
        P(),
        P("pipe", "dp", None),
        P("pipe", "dp", None),
        P("pipe", None),
        P(),
        P(None, "pipe"),
    )
    return jax.shard_map(
        on_device,
        mesh=mesh,
        in_specs=placed,
        out_specs=(P(None, "dp", "ctx", "pipe"), P("dp", "pipe")),
        check_vma=False,
    )
```

```python
import jax
import jax.numpy as jnp
from jax import lax
from jax.sharding import PartitionSpec as P

HEAD = 96


epsilon = 1e-06


def shifted(value, axis, steps):
    count = lax.axis_size(axis)
    first, last = (max(0, -steps), min(count, count - steps))
    return lax.ppermute(value, axis, [(source, source + steps) for source in range(first, last)])


def broadcast(value, axis, source):
    kept = jnp.where(lax.axis_index(axis) == source, value, 0).astype(value.dtype)
    return lax.psum(kept, axis)


def rms_scale(values, gain_row):
    return (
        values * lax.rsqrt(jnp.mean(values * values, axis=-1, keepdims=True) + epsilon) * gain_row
    )


def on_device(
    clean_latent,
    noise_latent,
    time_index,
    frame_ids,
    embed_weight,
    time_vector,
    query_weight,
    key_weight,
    norm_gain,
    head_gain,
    head_weight,
):
    phase_index = lax.axis_index("pipe")
    phase_count = lax.axis_size("pipe")
    cycle_size = lax.axis_size("ctx")
    micro_count = clean_latent.shape[0]
    local_rows = clean_latent.shape[2]
    model_width = embed_weight.shape[1]
    head_count = model_width // HEAD
    local_heads = head_count // cycle_size
    local_width = local_heads * HEAD
    seq_total = local_rows * cycle_size
    score_scale = HEAD ** (-0.5)
    flow_time = ((time_index.astype(jnp.float32) + 0.5) / 1000.0)[:, :, None, None]
    noisy_input = ((1.0 - flow_time) * noise_latent + flow_time * clean_latent).astype(jnp.bfloat16)
    target = clean_latent - noise_latent
    embedded = jnp.einsum(
        "mbsp,pd->mbsd", noisy_input, embed_weight, preferred_element_type=jnp.float32
    )
    embedded = (embedded + flow_time * time_vector).astype(jnp.bfloat16)
    dp_count = lax.axis_size("dp")
    column_start = lax.axis_index("ctx") * local_width

    def gather_whole(weight):
        piece = lax.dynamic_slice_in_dim(weight[0], column_start, local_width, 1)
        pieces = lax.all_gather(piece, ("dp", "ctx"), axis=0, tiled=False)
        rows = pieces.shape[1]
        return (
            pieces.reshape(dp_count, cycle_size, rows, local_width)
            .transpose(0, 2, 1, 3)
            .reshape(dp_count * rows, cycle_size * local_width)
        )

    full_query = gather_whole(query_weight)
    full_key = gather_whole(key_weight)
    head_full = lax.all_gather(head_weight, "pipe", axis=1, tiled=True)
    section_gain = norm_gain[0]

    def attention(by_heads, frame_row):
        query_all = by_heads[0].reshape(seq_total, local_heads, HEAD)
        key_all = by_heads[1].reshape(seq_total, local_heads, HEAD)
        value_all = by_heads[2].reshape(seq_total, local_heads, HEAD)
        allowed = frame_row[None, :] <= frame_row[:, None]
        scores = (
            jnp.einsum("shd,khd->hsk", query_all, key_all, preferred_element_type=jnp.float32)
            * score_scale
        )
        scores = jnp.where(allowed[None], scores, -1e30)
        row_max = jnp.max(scores, axis=-1, keepdims=True)
        weights = jnp.where(allowed[None], jnp.exp(scores - row_max), 0.0)
        row_sum = jnp.sum(weights, axis=-1)
        mixed = jnp.einsum(
            "hsk,khd->hsd",
            weights.astype(jnp.bfloat16),
            value_all,
            preferred_element_type=jnp.float32,
        ) / row_sum[..., None]
        return mixed.transpose(1, 0, 2).reshape(seq_total, local_width).astype(jnp.bfloat16)

    incoming = jnp.zeros((1, local_rows, model_width), jnp.bfloat16)
    finals = []
    moment_count = micro_count + phase_count - 1
    for moment in range(moment_count):
        micro_slot = jnp.clip(moment - phase_index, 0, micro_count - 1)
        active = jnp.logical_and(moment >= phase_index, moment - phase_index < micro_count)
        current = jnp.where(phase_index == 0, embedded[min(moment, micro_count - 1)], incoming)
        frame_row = lax.dynamic_index_in_dim(frame_ids, micro_slot, 0, keepdims=False)[0]
        wide_state = current.astype(jnp.float32)
        normed = rms_scale(wide_state, section_gain).astype(jnp.bfloat16)[0]

        def project(source):
            queries = jnp.dot(source, full_query, preferred_element_type=jnp.float32).astype(
                jnp.bfloat16
            )
            keys = jnp.dot(source, full_key, preferred_element_type=jnp.float32).astype(
                jnp.bfloat16
            )
            return jnp.stack((queries, keys, source), axis=0)

        def blank_triple(source):
            return jnp.zeros((3,) + source.shape, jnp.bfloat16)

        triple = lax.cond(active, project, blank_triple, normed)
        section_by_heads = lax.all_to_all(triple, "ctx", split_axis=2, concat_axis=1, tiled=True)

        def run_attention(arrived):
            return attention(arrived, frame_row)

        def blank_heads(arrived):
            return jnp.zeros((seq_total, local_width), jnp.bfloat16)

        mixed_heads = lax.cond(active, run_attention, blank_heads, section_by_heads)
        mixed = lax.all_to_all(mixed_heads, "ctx", split_axis=0, concat_axis=1, tiled=True)
        result = (wide_state + mixed.astype(jnp.float32)[None]).astype(jnp.bfloat16)
        if moment + 1 < moment_count:
            incoming = shifted(result, "pipe", 1)
        if moment >= phase_count - 1:
            finals.append(result)
    final_state = jnp.stack(finals, axis=0)
    last_phase = phase_count - 1
    is_last = phase_index == last_phase
    head_cols = head_weight.shape[1]
    final_norm = rms_scale(final_state.astype(jnp.float32), head_gain).astype(jnp.bfloat16)
    velocity_all = jnp.einsum(
        "mbsd,dp->mbsp", final_norm, head_full, preferred_element_type=jnp.float32
    )
    residue = velocity_all - target
    grad_all = jnp.einsum(
        "mbsd,mbsp->dp", final_norm.astype(jnp.float32), residue, precision=lax.Precision.HIGHEST
    ) / float(seq_total)
    grad_rows = lax.psum_scatter(grad_all, "dp", scatter_dimension=0, tiled=True)
    velocity_in = jnp.zeros(velocity_all.shape[:3] + (head_cols,), jnp.float32)
    gradient_in = jnp.zeros((grad_rows.shape[0], head_cols), jnp.float32)
    for target_phase in range(last_phase):
        cols = slice(target_phase * head_cols, (target_phase + 1) * head_cols)
        pair = [(last_phase, target_phase)]
        velocity_in = velocity_in + lax.ppermute(velocity_all[..., cols], "pipe", pair)
        gradient_in = gradient_in + lax.ppermute(grad_rows[:, cols], "pipe", pair)
    own_cols = slice(last_phase * head_cols, phase_count * head_cols)
    velocity = jnp.where(is_last, velocity_all[..., own_cols], velocity_in)
    gradient = lax.psum(jnp.where(is_last, grad_rows[:, own_cols], gradient_in), "ctx")
    return (velocity, gradient)


def solution(mesh):
    placed = (
        P(None, "dp", "ctx", None),
        P(None, "dp", "ctx", None),
        P(None, "dp"),
        P(None, "dp", None),
        P(),
        P(),
        P("pipe", "dp", None),
        P("pipe", "dp", None),
        P("pipe", None),
        P(),
        P(None, "pipe"),
    )
    return jax.shard_map(
        on_device,
        mesh=mesh,
        in_specs=placed,
        out_specs=(P(None, "dp", "ctx", "pipe"), P("dp", "pipe")),
        check_vma=False,
    )
```

```python
import jax
import jax.numpy as jnp
from jax import lax
from jax.sharding import PartitionSpec as P

HEAD = 96


epsilon = 1e-06


def shifted(value, axis, steps):
    count = lax.axis_size(axis)
    first, last = (max(0, -steps), min(count, count - steps))
    return lax.ppermute(value, axis, [(source, source + steps) for source in range(first, last)])


def rms_scale(values, gain_row):
    return (
        values * lax.rsqrt(jnp.mean(values * values, axis=-1, keepdims=True) + epsilon) * gain_row
    )


def on_device(
    clean_latent,
    noise_latent,
    time_index,
    frame_ids,
    embed_weight,
    time_vector,
    query_weight,
    key_weight,
    norm_gain,
    head_gain,
    head_weight,
):
    phase_index = lax.axis_index("pipe")
    phase_count = lax.axis_size("pipe")
    cycle_size = lax.axis_size("ctx")
    micro_count = clean_latent.shape[0]
    local_rows = clean_latent.shape[2]
    model_width = embed_weight.shape[1]
    head_count = model_width // HEAD
    local_heads = head_count // cycle_size
    local_width = local_heads * HEAD
    seq_total = local_rows * cycle_size
    score_scale = HEAD ** (-0.5)
    flow_time = ((time_index.astype(jnp.float32) + 0.5) / 1000.0)[:, :, None, None]
    noisy_input = ((1.0 - flow_time) * noise_latent + flow_time * clean_latent).astype(jnp.bfloat16)
    target = clean_latent - noise_latent
    embedded = jnp.einsum(
        "mbsp,pd->mbsd", noisy_input, embed_weight, preferred_element_type=jnp.float32
    )
    embedded = (embedded + flow_time * time_vector).astype(jnp.bfloat16)
    dp_index = lax.axis_index("dp")
    dp_count = lax.axis_size("dp")
    full_query = lax.all_gather(query_weight[0], "dp", axis=0, tiled=True)
    key_blocks = [key_weight[0]]
    for step in range(1, dp_count):
        pairs = [(source, (source + step) % dp_count) for source in range(dp_count)]
        key_blocks.append(lax.ppermute(key_weight[0], "dp", pairs))
    by_step = jnp.stack(key_blocks, axis=0)
    source_step = (dp_index - jnp.arange(dp_count, dtype=jnp.int32)) % dp_count
    full_key = jnp.take(by_step, source_step, axis=0).reshape(model_width, model_width)
    head_full = lax.all_gather(head_weight, "pipe", axis=1, tiled=True)
    section_gain = norm_gain[0]

    def attention(by_heads, frame_row):
        query_all = by_heads[0].reshape(seq_total, local_heads, HEAD)
        key_all = by_heads[1].reshape(seq_total, local_heads, HEAD)
        value_all = by_heads[2].reshape(seq_total, local_heads, HEAD)
        allowed = frame_row[None, :] <= frame_row[:, None]
        scores = (
            jnp.einsum("shd,khd->hsk", query_all, key_all, preferred_element_type=jnp.float32)
            * score_scale
        )
        scores = jnp.where(allowed[None], scores, -1e30)
        row_max = jnp.max(scores, axis=-1, keepdims=True)
        weights = jnp.where(allowed[None], jnp.exp(scores - row_max), 0.0)
        row_sum = jnp.sum(weights, axis=-1)
        mixed = jnp.einsum(
            "hsk,khd->hsd",
            weights.astype(jnp.bfloat16),
            value_all,
            preferred_element_type=jnp.float32,
        ) / row_sum[..., None]
        return mixed.transpose(1, 0, 2).reshape(seq_total, local_width).astype(jnp.bfloat16)

    incoming = jnp.zeros((1, local_rows, model_width), jnp.bfloat16)
    finals = []
    moment_count = micro_count + phase_count - 1
    for moment in range(moment_count):
        micro_slot = jnp.clip(moment - phase_index, 0, micro_count - 1)
        active = jnp.logical_and(moment >= phase_index, moment - phase_index < micro_count)
        current = jnp.where(phase_index == 0, embedded[min(moment, micro_count - 1)], incoming)
        frame_row = lax.dynamic_index_in_dim(frame_ids, micro_slot, 0, keepdims=False)[0]
        wide_state = current.astype(jnp.float32)
        normed = rms_scale(wide_state, section_gain).astype(jnp.bfloat16)[0]

        def project(source):
            queries = jnp.dot(source, full_query, preferred_element_type=jnp.float32).astype(
                jnp.bfloat16
            )
            keys = jnp.dot(source, full_key, preferred_element_type=jnp.float32).astype(
                jnp.bfloat16
            )
            return jnp.stack((queries, keys, source), axis=0)

        def blank_triple(source):
            return jnp.zeros((3,) + source.shape, jnp.bfloat16)

        triple = lax.cond(active, project, blank_triple, normed)
        section_by_heads = lax.all_to_all(triple, "ctx", split_axis=2, concat_axis=1, tiled=True)

        def run_attention(arrived):
            return attention(arrived, frame_row)

        def blank_heads(arrived):
            return jnp.zeros((seq_total, local_width), jnp.bfloat16)

        mixed_heads = lax.cond(active, run_attention, blank_heads, section_by_heads)
        mixed = lax.all_to_all(mixed_heads, "ctx", split_axis=0, concat_axis=1, tiled=True)
        result = (wide_state + mixed.astype(jnp.float32)[None]).astype(jnp.bfloat16)
        if moment + 1 < moment_count:
            incoming = shifted(result, "pipe", 1)
        if moment >= phase_count - 1:
            finals.append(result)
    final_state = jnp.stack(finals, axis=0)
    last_phase = phase_count - 1
    is_last = phase_index == last_phase
    head_cols = head_weight.shape[1]
    final_norm = rms_scale(final_state.astype(jnp.float32), head_gain).astype(jnp.bfloat16)
    velocity_all = jnp.einsum(
        "mbsd,dp->mbsp", final_norm, head_full, preferred_element_type=jnp.float32
    )
    residue = velocity_all - target
    grad_all = jnp.einsum(
        "mbsd,mbsp->dp", final_norm.astype(jnp.float32), residue, precision=lax.Precision.HIGHEST
    ) / float(seq_total)
    grad_rows = lax.psum_scatter(grad_all, "dp", scatter_dimension=0, tiled=True)
    grad_rows = lax.psum(grad_rows, "ctx")
    velocity_in = jnp.zeros(velocity_all.shape[:3] + (head_cols,), jnp.float32)
    gradient_in = jnp.zeros((grad_rows.shape[0], head_cols), jnp.float32)
    for target_phase in range(last_phase):
        cols = slice(target_phase * head_cols, (target_phase + 1) * head_cols)
        pair = [(last_phase, target_phase)]
        velocity_in = velocity_in + lax.ppermute(velocity_all[..., cols], "pipe", pair)
        gradient_in = gradient_in + lax.ppermute(grad_rows[:, cols], "pipe", pair)
    own_cols = slice(last_phase * head_cols, phase_count * head_cols)
    velocity = jnp.where(is_last, velocity_all[..., own_cols], velocity_in)
    gradient = jnp.where(is_last, grad_rows[:, own_cols], gradient_in)
    return (velocity, gradient)


def solution(mesh):
    placed = (
        P(None, "dp", "ctx", None),
        P(None, "dp", "ctx", None),
        P(None, "dp"),
        P(None, "dp", None),
        P(),
        P(),
        P("pipe", "dp", None),
        P("pipe", "dp", None),
        P("pipe", None),
        P(),
        P(None, "pipe"),
    )
    return jax.shard_map(
        on_device,
        mesh=mesh,
        in_specs=placed,
        out_specs=(P(None, "dp", "ctx", "pipe"), P("dp", "pipe")),
        check_vma=False,
    )
```

```python
import jax
import jax.numpy as jnp
from jax import lax
from jax.sharding import PartitionSpec as P

HEAD = 96


epsilon = 1e-06


def shifted(value, axis, steps):
    count = lax.axis_size(axis)
    first, last = (max(0, -steps), min(count, count - steps))
    return lax.ppermute(value, axis, [(source, source + steps) for source in range(first, last)])


def rms_scale(values, gain_row):
    return (
        values * lax.rsqrt(jnp.mean(values * values, axis=-1, keepdims=True) + epsilon) * gain_row
    )


def on_device(
    clean_latent,
    noise_latent,
    time_index,
    frame_ids,
    embed_weight,
    time_vector,
    query_weight,
    key_weight,
    norm_gain,
    head_gain,
    head_weight,
):
    phase_index = lax.axis_index("pipe")
    phase_count = lax.axis_size("pipe")
    cycle_size = lax.axis_size("ctx")
    micro_count = clean_latent.shape[0]
    local_rows = clean_latent.shape[2]
    model_width = embed_weight.shape[1]
    head_count = model_width // HEAD
    local_heads = head_count // cycle_size
    local_width = local_heads * HEAD
    seq_total = local_rows * cycle_size
    score_scale = HEAD ** (-0.5)
    flow_time = ((time_index.astype(jnp.float32) + 0.5) / 1000.0)[:, :, None, None]
    noisy_input = ((1.0 - flow_time) * noise_latent + flow_time * clean_latent).astype(jnp.bfloat16)
    target = clean_latent - noise_latent
    embedded = jnp.einsum(
        "mbsp,pd->mbsd", noisy_input, embed_weight, preferred_element_type=jnp.float32
    )
    embedded = (embedded + flow_time * time_vector).astype(jnp.bfloat16)
    dp_index = lax.axis_index("dp")
    dp_count = lax.axis_size("dp")
    source_step = (dp_index - jnp.arange(dp_count, dtype=jnp.int32)) % dp_count
    first_phases = list(range(0, phase_count, 2))
    later_phases = list(range(1, phase_count, 2))

    def gather_rows(block, phases):
        pieces = [block]
        for step in range(1, dp_count):
            pairs = [
                (phase * dp_count + source, phase * dp_count + (source + step) % dp_count)
                for phase in phases
                for source in range(dp_count)
            ]
            pieces.append(lax.ppermute(block, ("pipe", "dp"), pairs))
        by_step = jnp.stack(pieces, axis=0)
        by_source = jnp.take(by_step, source_step, axis=0)
        return by_source.transpose(1, 0, 2, 3).reshape(2, model_width, model_width)

    weight_block = jnp.stack((query_weight[0], key_weight[0]), axis=0)
    early_weights = gather_rows(weight_block, first_phases)
    takes_early = phase_index % 2 == 0
    ready_pairs = [(phase, phase + 1) for phase in first_phases if phase + 1 < phase_count]
    ready = lax.ppermute(early_weights[0, :8, :128], "pipe", ready_pairs)
    late_block, ready = lax.optimization_barrier((weight_block, ready))
    late_weights = gather_rows(late_block, later_phases)
    last_phase = phase_count - 1
    head_pieces = []
    for source_phase in range(phase_count):
        if source_phase == last_phase:
            head_pieces.append(head_weight)
        else:
            head_pieces.append(lax.ppermute(head_weight, "pipe", [(source_phase, last_phase)]))
    head_full = jnp.concatenate(head_pieces, axis=1)
    section_gain = norm_gain[0]

    def attention(by_heads, frame_row):
        query_all = by_heads[0].reshape(seq_total, local_heads, HEAD)
        key_all = by_heads[1].reshape(seq_total, local_heads, HEAD)
        value_all = by_heads[2].reshape(seq_total, local_heads, HEAD)
        allowed = frame_row[None, :] <= frame_row[:, None]
        scores = (
            jnp.einsum("shd,khd->hsk", query_all, key_all, preferred_element_type=jnp.float32)
            * score_scale
        )
        scores = jnp.where(allowed[None], scores, -1e30)
        row_max = jnp.max(scores, axis=-1, keepdims=True)
        weights = jnp.where(allowed[None], jnp.exp(scores - row_max), 0.0)
        row_sum = jnp.sum(weights, axis=-1)
        mixed = jnp.einsum(
            "hsk,khd->hsd",
            weights.astype(jnp.bfloat16),
            value_all,
            preferred_element_type=jnp.float32,
        ) / row_sum[..., None]
        return mixed.transpose(1, 0, 2).reshape(seq_total, local_width).astype(jnp.bfloat16)

    incoming = jnp.zeros((1, local_rows, model_width), jnp.bfloat16)
    finals = []
    moment_count = micro_count + phase_count - 1
    for moment in range(moment_count):
        micro_slot = jnp.clip(moment - phase_index, 0, micro_count - 1)
        active = jnp.logical_and(moment >= phase_index, moment - phase_index < micro_count)
        current = jnp.where(phase_index == 0, embedded[min(moment, micro_count - 1)], incoming)
        frame_row = lax.dynamic_index_in_dim(frame_ids, micro_slot, 0, keepdims=False)[0]
        wide_state = current.astype(jnp.float32)
        normed = rms_scale(wide_state, section_gain).astype(jnp.bfloat16)[0]

        if moment == 0:
            weights_now = early_weights
        else:
            weights_now = jnp.where(takes_early, early_weights, late_weights)

        def project(source, weights_now=weights_now):
            queries = jnp.dot(source, weights_now[0], preferred_element_type=jnp.float32).astype(
                jnp.bfloat16
            )
            keys = jnp.dot(source, weights_now[1], preferred_element_type=jnp.float32).astype(
                jnp.bfloat16
            )
            return jnp.stack((queries, keys, source), axis=0)

        def blank_triple(source):
            return jnp.zeros((3,) + source.shape, jnp.bfloat16)

        triple = lax.cond(active, project, blank_triple, normed)
        section_by_heads = lax.all_to_all(triple, "ctx", split_axis=2, concat_axis=1, tiled=True)

        def run_attention(arrived):
            return attention(arrived, frame_row)

        def blank_heads(arrived):
            return jnp.zeros((seq_total, local_width), jnp.bfloat16)

        mixed_heads = lax.cond(active, run_attention, blank_heads, section_by_heads)
        mixed = lax.all_to_all(mixed_heads, "ctx", split_axis=0, concat_axis=1, tiled=True)
        result = (wide_state + mixed.astype(jnp.float32)[None]).astype(jnp.bfloat16)
        if moment + 1 < moment_count:
            incoming = shifted(result, "pipe", 1)
        if moment >= phase_count - 1:
            finals.append(result)
    final_state = jnp.stack(finals, axis=0)
    is_last = phase_index == last_phase
    head_cols = head_weight.shape[1]
    final_norm = rms_scale(final_state.astype(jnp.float32), head_gain).astype(jnp.bfloat16)
    velocity_all = jnp.einsum(
        "mbsd,dp->mbsp", final_norm, head_full, preferred_element_type=jnp.float32
    )
    residue = velocity_all - target
    grad_all = jnp.einsum(
        "mbsd,mbsp->dp", final_norm.astype(jnp.float32), residue, precision=lax.Precision.HIGHEST
    ) / float(seq_total)
    grad_rows = lax.psum_scatter(grad_all, "dp", scatter_dimension=0, tiled=True)
    grad_rows = lax.psum(grad_rows, "ctx")
    velocity_in = jnp.zeros(velocity_all.shape[:3] + (head_cols,), jnp.float32)
    gradient_in = jnp.zeros((grad_rows.shape[0], head_cols), jnp.float32)
    for target_phase in range(last_phase):
        cols = slice(target_phase * head_cols, (target_phase + 1) * head_cols)
        pair = [(last_phase, target_phase)]
        velocity_in = velocity_in + lax.ppermute(velocity_all[..., cols], "pipe", pair)
        gradient_in = gradient_in + lax.ppermute(grad_rows[:, cols], "pipe", pair)
    own_cols = slice(last_phase * head_cols, phase_count * head_cols)
    velocity = jnp.where(is_last, velocity_all[..., own_cols], velocity_in)
    gradient = jnp.where(is_last, grad_rows[:, own_cols], gradient_in)
    return (velocity, gradient)


def solution(mesh):
    placed = (
        P(None, "dp", "ctx", None),
        P(None, "dp", "ctx", None),
        P(None, "dp"),
        P(None, "dp", None),
        P(),
        P(),
        P("pipe", "dp", None),
        P("pipe", "dp", None),
        P("pipe", None),
        P(),
        P(None, "pipe"),
    )
    return jax.shard_map(
        on_device,
        mesh=mesh,
        in_specs=placed,
        out_specs=(P(None, "dp", "ctx", "pipe"), P("dp", "pipe")),
        check_vma=False,
    )
```

```python
import jax
import jax.numpy as jnp
from jax import lax
from jax.sharding import PartitionSpec as P

HEAD = 96


epsilon = 1e-06


def shifted(value, axis, steps):
    count = lax.axis_size(axis)
    first, last = (max(0, -steps), min(count, count - steps))
    return lax.ppermute(value, axis, [(source, source + steps) for source in range(first, last)])


def rms_scale(values, gain_row):
    return (
        values * lax.rsqrt(jnp.mean(values * values, axis=-1, keepdims=True) + epsilon) * gain_row
    )


def on_device(
    clean_latent,
    noise_latent,
    time_index,
    frame_ids,
    embed_weight,
    time_vector,
    query_weight,
    key_weight,
    norm_gain,
    head_gain,
    head_weight,
):
    phase_index = lax.axis_index("pipe")
    phase_count = lax.axis_size("pipe")
    cycle_size = lax.axis_size("ctx")
    micro_count = clean_latent.shape[0]
    local_rows = clean_latent.shape[2]
    model_width = embed_weight.shape[1]
    head_count = model_width // HEAD
    local_heads = head_count // cycle_size
    local_width = local_heads * HEAD
    seq_total = local_rows * cycle_size
    score_scale = HEAD ** (-0.5)
    flow_time = ((time_index.astype(jnp.float32) + 0.5) / 1000.0)[:, :, None, None]
    noisy_input = ((1.0 - flow_time) * noise_latent + flow_time * clean_latent).astype(jnp.bfloat16)
    target = clean_latent - noise_latent
    embedded = jnp.einsum(
        "mbsp,pd->mbsd", noisy_input, embed_weight, preferred_element_type=jnp.float32
    )
    embedded = (embedded + flow_time * time_vector).astype(jnp.bfloat16)
    dp_index = lax.axis_index("dp")
    dp_count = lax.axis_size("dp")
    full_query = lax.all_gather(query_weight[0], "dp", axis=0, tiled=True)
    key_blocks = [key_weight[0]]
    for step in range(1, dp_count):
        pairs = [(source, (source + step) % dp_count) for source in range(dp_count)]
        key_blocks.append(lax.ppermute(key_weight[0], "dp", pairs))
    key_by_step = jnp.stack(key_blocks, axis=0).reshape(model_width, model_width)
    source_block = (dp_index - jnp.arange(dp_count, dtype=jnp.int32)) % dp_count
    last_phase = phase_count - 1
    head_pieces = []
    for source_phase in range(phase_count):
        if source_phase == last_phase:
            head_pieces.append(head_weight)
        else:
            head_pieces.append(lax.ppermute(head_weight, "pipe", [(source_phase, last_phase)]))
    head_full = jnp.concatenate(head_pieces, axis=1)
    section_gain = norm_gain[0]

    def attention(by_heads, frame_row):
        query_all = by_heads[0].reshape(seq_total, local_heads, HEAD)
        key_all = by_heads[1].reshape(seq_total, local_heads, HEAD)
        value_all = by_heads[2].reshape(seq_total, local_heads, HEAD)
        allowed = frame_row[None, :] <= frame_row[:, None]
        scores = (
            jnp.einsum("shd,khd->hsk", query_all, key_all, preferred_element_type=jnp.float32)
            * score_scale
        )
        scores = jnp.where(allowed[None], scores, -1e30)
        row_max = jnp.max(scores, axis=-1, keepdims=True)
        weights = jnp.where(allowed[None], jnp.exp(scores - row_max), 0.0)
        row_sum = jnp.sum(weights, axis=-1)
        mixed = jnp.einsum(
            "hsk,khd->hsd",
            weights.astype(jnp.bfloat16),
            value_all,
            preferred_element_type=jnp.float32,
        ) / row_sum[..., None]
        return mixed.transpose(1, 0, 2).reshape(seq_total, local_width).astype(jnp.bfloat16)

    incoming = jnp.zeros((1, local_rows, model_width), jnp.bfloat16)
    finals = []
    moment_count = micro_count + phase_count - 1
    for moment in range(moment_count):
        micro_slot = jnp.clip(moment - phase_index, 0, micro_count - 1)
        active = jnp.logical_and(moment >= phase_index, moment - phase_index < micro_count)
        current = jnp.where(phase_index == 0, embedded[min(moment, micro_count - 1)], incoming)
        frame_row = lax.dynamic_index_in_dim(frame_ids, micro_slot, 0, keepdims=False)[0]
        wide_state = current.astype(jnp.float32)
        normed = rms_scale(wide_state, section_gain).astype(jnp.bfloat16)[0]

        def project(source):
            queries = jnp.dot(source, full_query, preferred_element_type=jnp.float32).astype(
                jnp.bfloat16
            )
            block_rows = model_width // dp_count
            by_block = source.reshape(local_rows, dp_count, block_rows)
            in_step_order = jnp.take(by_block, source_block, axis=1).reshape(local_rows, model_width)
            keys = jnp.dot(in_step_order, key_by_step, preferred_element_type=jnp.float32).astype(
                jnp.bfloat16
            )
            return jnp.stack((queries, keys, source), axis=0)

        def blank_triple(source):
            return jnp.zeros((3,) + source.shape, jnp.bfloat16)

        triple = lax.cond(active, project, blank_triple, normed)
        section_by_heads = lax.all_to_all(triple, "ctx", split_axis=2, concat_axis=1, tiled=True)

        def run_attention(arrived):
            return attention(arrived, frame_row)

        def blank_heads(arrived):
            return jnp.zeros((seq_total, local_width), jnp.bfloat16)

        mixed_heads = lax.cond(active, run_attention, blank_heads, section_by_heads)
        mixed = lax.all_to_all(mixed_heads, "ctx", split_axis=0, concat_axis=1, tiled=True)
        result = (wide_state + mixed.astype(jnp.float32)[None]).astype(jnp.bfloat16)
        if moment + 1 < moment_count:
            incoming = shifted(result, "pipe", 1)
        if moment >= phase_count - 1:
            finals.append(result)
    final_state = jnp.stack(finals, axis=0)
    is_last = phase_index == last_phase
    head_cols = head_weight.shape[1]
    final_norm = rms_scale(final_state.astype(jnp.float32), head_gain).astype(jnp.bfloat16)
    velocity_all = jnp.einsum(
        "mbsd,dp->mbsp", final_norm, head_full, preferred_element_type=jnp.float32
    )
    residue = velocity_all - target
    grad_all = jnp.einsum(
        "mbsd,mbsp->dp", final_norm.astype(jnp.float32), residue, precision=lax.Precision.HIGHEST
    ) / float(seq_total)
    grad_rows = lax.psum_scatter(grad_all, "dp", scatter_dimension=0, tiled=True)
    grad_rows = lax.psum(grad_rows, "ctx")
    velocity_in = jnp.zeros(velocity_all.shape[:3] + (head_cols,), jnp.float32)
    gradient_in = jnp.zeros((grad_rows.shape[0], head_cols), jnp.float32)
    for target_phase in range(last_phase):
        cols = slice(target_phase * head_cols, (target_phase + 1) * head_cols)
        pair = [(last_phase, target_phase)]
        velocity_in = velocity_in + lax.ppermute(velocity_all[..., cols], "pipe", pair)
        gradient_in = gradient_in + lax.ppermute(grad_rows[:, cols], "pipe", pair)
    own_cols = slice(last_phase * head_cols, phase_count * head_cols)
    velocity = jnp.where(is_last, velocity_all[..., own_cols], velocity_in)
    gradient = jnp.where(is_last, grad_rows[:, own_cols], gradient_in)
    return (velocity, gradient)


def solution(mesh):
    placed = (
        P(None, "dp", "ctx", None),
        P(None, "dp", "ctx", None),
        P(None, "dp"),
        P(None, "dp", None),
        P(),
        P(),
        P("pipe", "dp", None),
        P("pipe", "dp", None),
        P("pipe", None),
        P(),
        P(None, "pipe"),
    )
    return jax.shard_map(
        on_device,
        mesh=mesh,
        in_specs=placed,
        out_specs=(P(None, "dp", "ctx", "pipe"), P("dp", "pipe")),
        check_vma=False,
    )
```

```python
import jax
import jax.numpy as jnp
from jax import lax
from jax.sharding import PartitionSpec as P

HEAD = 96


epsilon = 1e-06


def shifted(value, axis, steps):
    count = lax.axis_size(axis)
    first, last = (max(0, -steps), min(count, count - steps))
    return lax.ppermute(value, axis, [(source, source + steps) for source in range(first, last)])


def rms_scale(values, gain_row):
    return (
        values * lax.rsqrt(jnp.mean(values * values, axis=-1, keepdims=True) + epsilon) * gain_row
    )


def on_device(
    clean_latent,
    noise_latent,
    time_index,
    frame_ids,
    embed_weight,
    time_vector,
    query_weight,
    key_weight,
    norm_gain,
    head_gain,
    head_weight,
):
    phase_index = lax.axis_index("pipe")
    phase_count = lax.axis_size("pipe")
    cycle_size = lax.axis_size("ctx")
    micro_count = clean_latent.shape[0]
    local_rows = clean_latent.shape[2]
    model_width = embed_weight.shape[1]
    head_count = model_width // HEAD
    local_heads = head_count // cycle_size
    local_width = local_heads * HEAD
    seq_total = local_rows * cycle_size
    score_scale = HEAD ** (-0.5)
    flow_time = ((time_index.astype(jnp.float32) + 0.5) / 1000.0)[:, :, None, None]
    noisy_input = ((1.0 - flow_time) * noise_latent + flow_time * clean_latent).astype(jnp.bfloat16)
    target = clean_latent - noise_latent
    embedded = jnp.einsum(
        "mbsp,pd->mbsd", noisy_input, embed_weight, preferred_element_type=jnp.float32
    )
    embedded = (embedded + flow_time * time_vector).astype(jnp.bfloat16)
    dp_index = lax.axis_index("dp")
    dp_count = lax.axis_size("dp")
    full_query = lax.all_gather(query_weight[0], "dp", axis=0, tiled=True)
    key_blocks = [key_weight[0]]
    for step in range(1, dp_count):
        pairs = [(source, (source + step) % dp_count) for source in range(dp_count)]
        key_blocks.append(lax.ppermute(key_weight[0], "dp", pairs))
    key_by_step = jnp.stack(key_blocks, axis=0).reshape(model_width, model_width)
    source_block = (dp_index - jnp.arange(dp_count, dtype=jnp.int32)) % dp_count
    last_phase = phase_count - 1
    head_pieces = []
    for source_phase in range(phase_count):
        if source_phase == last_phase:
            head_pieces.append(head_weight)
        else:
            head_pieces.append(lax.ppermute(head_weight, "pipe", [(source_phase, last_phase)]))
    head_full = jnp.concatenate(head_pieces, axis=1)
    section_gain = norm_gain[0]

    def attention(by_heads, frame_row):
        query_all = by_heads[0].reshape(seq_total, local_heads, HEAD)
        key_all = by_heads[1].reshape(seq_total, local_heads, HEAD)
        value_all = by_heads[2].reshape(seq_total, local_heads, HEAD)
        allowed = frame_row[None, :] <= frame_row[:, None]
        scores = (
            jnp.einsum("shd,khd->hsk", query_all, key_all, preferred_element_type=jnp.float32)
            * score_scale
        )
        scores = jnp.where(allowed[None], scores, -1e30)
        row_max = jnp.max(scores, axis=-1, keepdims=True)
        weights = jnp.where(allowed[None], jnp.exp(scores - row_max), 0.0)
        row_sum = jnp.sum(weights, axis=-1)
        mixed = jnp.einsum(
            "hsk,khd->hsd",
            weights.astype(jnp.bfloat16),
            value_all,
            preferred_element_type=jnp.float32,
        ) / row_sum[..., None]
        return mixed.transpose(1, 0, 2).reshape(seq_total, local_width).astype(jnp.bfloat16)

    incoming = jnp.zeros((1, local_rows, model_width), jnp.bfloat16)
    finals = []
    moment_count = micro_count + phase_count - 1
    for moment in range(moment_count):
        micro_slot = jnp.clip(moment - phase_index, 0, micro_count - 1)
        active = jnp.logical_and(moment >= phase_index, moment - phase_index < micro_count)
        current = jnp.where(phase_index == 0, embedded[min(moment, micro_count - 1)], incoming)
        frame_row = lax.dynamic_index_in_dim(frame_ids, micro_slot, 0, keepdims=False)[0]
        wide_state = current.astype(jnp.float32)
        normed = rms_scale(wide_state, section_gain).astype(jnp.bfloat16)[0]

        def project(source):
            queries = jnp.dot(source, full_query, preferred_element_type=jnp.float32).astype(
                jnp.bfloat16
            )
            block_rows = model_width // dp_count
            by_block = source.reshape(local_rows, dp_count, block_rows)
            in_step_order = jnp.take(by_block, source_block, axis=1).reshape(local_rows, model_width)
            keys = jnp.dot(in_step_order, key_by_step, preferred_element_type=jnp.float32).astype(
                jnp.bfloat16
            )
            return jnp.stack((queries, keys, source), axis=0)

        def blank_triple(source):
            return jnp.zeros((3,) + source.shape, jnp.bfloat16)

        triple = lax.cond(active, project, blank_triple, normed)
        section_by_heads = lax.all_to_all(triple, "ctx", split_axis=2, concat_axis=1, tiled=True)

        def run_attention(arrived):
            return attention(arrived, frame_row)

        def blank_heads(arrived):
            return jnp.zeros((seq_total, local_width), jnp.bfloat16)

        mixed_heads = lax.cond(active, run_attention, blank_heads, section_by_heads)
        mixed = lax.all_to_all(mixed_heads, "ctx", split_axis=0, concat_axis=1, tiled=True)
        result = (wide_state + mixed.astype(jnp.float32)[None]).astype(jnp.bfloat16)
        if moment + 1 < moment_count:
            incoming = shifted(result, "pipe", 1)
        if moment >= phase_count - 1:
            finals.append(result)
    final_state = jnp.stack(finals, axis=0)
    is_last = phase_index == last_phase
    head_cols = head_weight.shape[1]
    final_norm = rms_scale(final_state.astype(jnp.float32), head_gain).astype(jnp.bfloat16)
    velocity_all = jnp.einsum(
        "mbsd,dp->mbsp", final_norm, head_full, preferred_element_type=jnp.float32
    )
    residue = velocity_all - target
    grad_all = jnp.einsum(
        "mbsd,mbsp->dp", final_norm.astype(jnp.float32), residue, precision=lax.Precision.HIGHEST
    ) / float(seq_total)
    velocity_in = jnp.zeros(velocity_all.shape[:3] + (head_cols,), jnp.float32)
    gradient_in = jnp.zeros((model_width, head_cols), jnp.float32)
    for target_phase in range(last_phase):
        cols = slice(target_phase * head_cols, (target_phase + 1) * head_cols)
        pair = [(last_phase, target_phase)]
        velocity_in = velocity_in + lax.ppermute(velocity_all[..., cols], "pipe", pair)
        gradient_in = gradient_in + lax.ppermute(grad_all[:, cols], "pipe", pair)
    own_cols = slice(last_phase * head_cols, phase_count * head_cols)
    velocity = jnp.where(is_last, velocity_all[..., own_cols], velocity_in)
    gradient_cols = jnp.where(is_last, grad_all[:, own_cols], gradient_in)
    gradient_rows = lax.psum_scatter(gradient_cols, "dp", scatter_dimension=0, tiled=True)
    gradient = lax.psum(gradient_rows, "ctx")
    return (velocity, gradient)


def solution(mesh):
    placed = (
        P(None, "dp", "ctx", None),
        P(None, "dp", "ctx", None),
        P(None, "dp"),
        P(None, "dp", None),
        P(),
        P(),
        P("pipe", "dp", None),
        P("pipe", "dp", None),
        P("pipe", None),
        P(),
        P(None, "pipe"),
    )
    return jax.shard_map(
        on_device,
        mesh=mesh,
        in_specs=placed,
        out_specs=(P(None, "dp", "ctx", "pipe"), P("dp", "pipe")),
        check_vma=False,
    )
```

```python
import jax
import jax.numpy as jnp
from jax import lax
from jax.sharding import PartitionSpec as P

HEAD = 96


epsilon = 1e-06


def shifted(value, axis, steps):
    count = lax.axis_size(axis)
    first, last = (max(0, -steps), min(count, count - steps))
    return lax.ppermute(value, axis, [(source, source + steps) for source in range(first, last)])


def rms_scale(values, gain_row):
    return (
        values * lax.rsqrt(jnp.mean(values * values, axis=-1, keepdims=True) + epsilon) * gain_row
    )


def on_device(
    clean_latent,
    noise_latent,
    time_index,
    frame_ids,
    embed_weight,
    time_vector,
    query_weight,
    key_weight,
    norm_gain,
    head_gain,
    head_weight,
):
    phase_index = lax.axis_index("pipe")
    phase_count = lax.axis_size("pipe")
    cycle_size = lax.axis_size("ctx")
    micro_count = clean_latent.shape[0]
    local_rows = clean_latent.shape[2]
    model_width = embed_weight.shape[1]
    head_count = model_width // HEAD
    local_heads = head_count // cycle_size
    local_width = local_heads * HEAD
    seq_total = local_rows * cycle_size
    score_scale = HEAD ** (-0.5)
    flow_time = ((time_index.astype(jnp.float32) + 0.5) / 1000.0)[:, :, None, None]
    noisy_input = ((1.0 - flow_time) * noise_latent + flow_time * clean_latent).astype(jnp.bfloat16)
    target = clean_latent - noise_latent
    embedded = jnp.einsum(
        "mbsp,pd->mbsd", noisy_input, embed_weight, preferred_element_type=jnp.float32
    )
    embedded = (embedded + flow_time * time_vector).astype(jnp.bfloat16)
    dp_index = lax.axis_index("dp")
    dp_count = lax.axis_size("dp")
    full_query = lax.all_gather(query_weight[0], "dp", axis=0, tiled=True)
    key_blocks = [key_weight[0]]
    for step in range(1, dp_count):
        pairs = [(source, (source + step) % dp_count) for source in range(dp_count)]
        key_blocks.append(lax.ppermute(key_weight[0], "dp", pairs))
    key_by_step = jnp.stack(key_blocks, axis=0).reshape(model_width, model_width)
    source_block = (dp_index - jnp.arange(dp_count, dtype=jnp.int32)) % dp_count
    last_phase = phase_count - 1
    head_pieces = []
    for source_phase in range(phase_count):
        if source_phase == last_phase:
            head_pieces.append(head_weight)
        else:
            head_pieces.append(lax.ppermute(head_weight, "pipe", [(source_phase, last_phase)]))
    head_full = jnp.concatenate(head_pieces, axis=1)
    section_gain = norm_gain[0]

    def attention(by_heads, frame_row):
        query_all = by_heads[0].reshape(seq_total, local_heads, HEAD)
        key_all = by_heads[1].reshape(seq_total, local_heads, HEAD)
        value_all = by_heads[2].reshape(seq_total, local_heads, HEAD)
        allowed = frame_row[None, :] <= frame_row[:, None]
        scores = (
            jnp.einsum("shd,khd->hsk", query_all, key_all, preferred_element_type=jnp.float32)
            * score_scale
        )
        scores = jnp.where(allowed[None], scores, -1e30)
        row_max = jnp.max(scores, axis=-1, keepdims=True)
        weights = jnp.where(allowed[None], jnp.exp(scores - row_max), 0.0)
        row_sum = jnp.sum(weights, axis=-1)
        mixed = jnp.einsum(
            "hsk,khd->hsd",
            weights.astype(jnp.bfloat16),
            value_all,
            preferred_element_type=jnp.float32,
        ) / row_sum[..., None]
        return mixed.transpose(1, 0, 2).reshape(seq_total, local_width).astype(jnp.bfloat16)

    incoming = jnp.zeros((1, local_rows, model_width), jnp.bfloat16)
    finals = []
    moment_count = micro_count + phase_count - 1
    for moment in range(moment_count):
        micro_slot = jnp.clip(moment - phase_index, 0, micro_count - 1)
        active = jnp.logical_and(moment >= phase_index, moment - phase_index < micro_count)
        current = jnp.where(phase_index == 0, embedded[min(moment, micro_count - 1)], incoming)
        frame_row = lax.dynamic_index_in_dim(frame_ids, micro_slot, 0, keepdims=False)[0]
        wide_state = current.astype(jnp.float32)
        normed = rms_scale(wide_state, section_gain).astype(jnp.bfloat16)[0]

        def project(source):
            queries = jnp.dot(source, full_query, preferred_element_type=jnp.float32).astype(
                jnp.bfloat16
            )
            block_rows = model_width // dp_count
            by_block = source.reshape(local_rows, dp_count, block_rows)
            in_step_order = jnp.take(by_block, source_block, axis=1).reshape(local_rows, model_width)
            keys = jnp.dot(in_step_order, key_by_step, preferred_element_type=jnp.float32).astype(
                jnp.bfloat16
            )
            return jnp.stack((queries, keys, source), axis=0)

        def blank_triple(source):
            return jnp.zeros((3,) + source.shape, jnp.bfloat16)

        triple = lax.cond(active, project, blank_triple, normed)
        section_by_heads = lax.all_to_all(triple, "ctx", split_axis=2, concat_axis=1, tiled=True)

        def run_attention(arrived):
            return attention(arrived, frame_row)

        def blank_heads(arrived):
            return jnp.zeros((seq_total, local_width), jnp.bfloat16)

        mixed_heads = lax.cond(active, run_attention, blank_heads, section_by_heads)
        mixed = lax.all_to_all(mixed_heads, "ctx", split_axis=0, concat_axis=1, tiled=True)
        result = (wide_state + mixed.astype(jnp.float32)[None]).astype(jnp.bfloat16)
        if moment + 1 < moment_count:
            incoming = shifted(result, "pipe", 1)
        if moment >= phase_count - 1:
            finals.append(result)
    final_state = jnp.stack(finals, axis=0)
    is_last = phase_index == last_phase
    head_cols = head_weight.shape[1]
    final_norm = rms_scale(final_state.astype(jnp.float32), head_gain).astype(jnp.bfloat16)
    velocity_all = jnp.einsum(
        "mbsd,dp->mbsp", final_norm, head_full, preferred_element_type=jnp.float32
    )
    residue = velocity_all - target
    grad_all = jnp.einsum(
        "mbsd,mbsp->dp", final_norm.astype(jnp.float32), residue, precision=lax.Precision.HIGHEST
    ) / float(seq_total)
    velocity_in = jnp.zeros(velocity_all.shape[:3] + (head_cols,), jnp.float32)
    for target_phase in range(last_phase):
        cols = slice(target_phase * head_cols, (target_phase + 1) * head_cols)
        pair = [(last_phase, target_phase)]
        velocity_in = velocity_in + lax.ppermute(velocity_all[..., cols], "pipe", pair)
    own_cols = slice(last_phase * head_cols, phase_count * head_cols)
    velocity = jnp.where(is_last, velocity_all[..., own_cols], velocity_in)
    grad_rows = lax.psum_scatter(grad_all, "dp", scatter_dimension=0, tiled=True)
    grad_rows = lax.psum(jnp.where(is_last, grad_rows, 0.0), ("ctx", "pipe"))
    gradient = lax.dynamic_slice_in_dim(grad_rows, phase_index * head_cols, head_cols, 1)
    return (velocity, gradient)


def solution(mesh):
    placed = (
        P(None, "dp", "ctx", None),
        P(None, "dp", "ctx", None),
        P(None, "dp"),
        P(None, "dp", None),
        P(),
        P(),
        P("pipe", "dp", None),
        P("pipe", "dp", None),
        P("pipe", None),
        P(),
        P(None, "pipe"),
    )
    return jax.shard_map(
        on_device,
        mesh=mesh,
        in_specs=placed,
        out_specs=(P(None, "dp", "ctx", "pipe"), P("dp", "pipe")),
        check_vma=False,
    )
```

```python
import jax
import jax.numpy as jnp
from jax import lax
from jax.sharding import PartitionSpec as P

HEAD = 96


epsilon = 1e-06


def shifted(value, axis, steps):
    count = lax.axis_size(axis)
    first, last = (max(0, -steps), min(count, count - steps))
    return lax.ppermute(value, axis, [(source, source + steps) for source in range(first, last)])


def rms_scale(values, gain_row):
    return (
        values * lax.rsqrt(jnp.mean(values * values, axis=-1, keepdims=True) + epsilon) * gain_row
    )


def on_device(
    clean_latent,
    noise_latent,
    time_index,
    frame_ids,
    embed_weight,
    time_vector,
    query_weight,
    key_weight,
    norm_gain,
    head_gain,
    head_weight,
):
    phase_index = lax.axis_index("pipe")
    phase_count = lax.axis_size("pipe")
    cycle_size = lax.axis_size("ctx")
    micro_count = clean_latent.shape[0]
    local_rows = clean_latent.shape[2]
    model_width = embed_weight.shape[1]
    head_count = model_width // HEAD
    local_heads = head_count // cycle_size
    local_width = local_heads * HEAD
    seq_total = local_rows * cycle_size
    score_scale = HEAD ** (-0.5)
    flow_time = ((time_index.astype(jnp.float32) + 0.5) / 1000.0)[:, :, None, None]
    noisy_input = ((1.0 - flow_time) * noise_latent + flow_time * clean_latent).astype(jnp.bfloat16)
    target = clean_latent - noise_latent
    embedded = jnp.einsum(
        "mbsp,pd->mbsd", noisy_input, embed_weight, preferred_element_type=jnp.float32
    )
    embedded = (embedded + flow_time * time_vector).astype(jnp.bfloat16)
    dp_index = lax.axis_index("dp")
    dp_count = lax.axis_size("dp")
    full_query = lax.all_gather(query_weight[0], "dp", axis=0, tiled=True)
    key_blocks = [key_weight[0]]
    for step in range(1, dp_count):
        pairs = [(source, (source + step) % dp_count) for source in range(dp_count)]
        key_blocks.append(lax.ppermute(key_weight[0], "dp", pairs))
    by_step = jnp.stack(key_blocks, axis=0)
    source_step = (dp_index - jnp.arange(dp_count, dtype=jnp.int32)) % dp_count
    full_key = jnp.take(by_step, source_step, axis=0).reshape(model_width, model_width)
    head_full = lax.all_gather(head_weight, "pipe", axis=1, tiled=True)
    section_gain = norm_gain[0]

    def attention(by_heads, frame_row):
        query_all = by_heads[0].reshape(seq_total, local_heads, HEAD)
        key_all = by_heads[1].reshape(seq_total, local_heads, HEAD)
        value_all = by_heads[2].reshape(seq_total, local_heads, HEAD)
        allowed = frame_row[None, :] <= frame_row[:, None]
        scores = (
            jnp.einsum("shd,khd->hsk", query_all, key_all, preferred_element_type=jnp.float32)
            * score_scale
        )
        scores = jnp.where(allowed[None], scores, -1e30)
        row_max = jnp.max(scores, axis=-1, keepdims=True)
        weights = jnp.where(allowed[None], jnp.exp(scores - row_max), 0.0)
        row_sum = jnp.sum(weights, axis=-1)
        mixed = jnp.einsum(
            "hsk,khd->hsd",
            weights.astype(jnp.bfloat16),
            value_all,
            preferred_element_type=jnp.float32,
        ) / row_sum[..., None]
        return mixed.transpose(1, 0, 2).reshape(seq_total, local_width).astype(jnp.bfloat16)

    incoming = jnp.zeros((1, local_rows, model_width), jnp.bfloat16)
    finals = []
    moment_count = micro_count + phase_count - 1
    for moment in range(moment_count):
        micro_slot = jnp.clip(moment - phase_index, 0, micro_count - 1)
        active = jnp.logical_and(moment >= phase_index, moment - phase_index < micro_count)
        current = jnp.where(phase_index == 0, embedded[min(moment, micro_count - 1)], incoming)
        frame_row = lax.dynamic_index_in_dim(frame_ids, micro_slot, 0, keepdims=False)[0]
        wide_state = current.astype(jnp.float32)
        normed = rms_scale(wide_state, section_gain).astype(jnp.bfloat16)[0]

        def project(source):
            queries = jnp.dot(source, full_query, preferred_element_type=jnp.float32).astype(
                jnp.bfloat16
            )
            keys = jnp.dot(source, full_key, preferred_element_type=jnp.float32).astype(
                jnp.bfloat16
            )
            return jnp.stack((queries, keys, source), axis=0)

        def blank_triple(source):
            return jnp.zeros((3,) + source.shape, jnp.bfloat16)

        triple = lax.cond(active, project, blank_triple, normed)
        section_by_heads = lax.all_to_all(triple, "ctx", split_axis=2, concat_axis=1, tiled=True)

        def run_attention(arrived):
            return attention(arrived, frame_row)

        def blank_heads(arrived):
            return jnp.zeros((seq_total, local_width), jnp.bfloat16)

        mixed_heads = lax.cond(active, run_attention, blank_heads, section_by_heads)
        chunk = local_rows * local_width
        lanes = 128 if chunk % 128 == 0 else chunk
        outgoing = mixed_heads.reshape(cycle_size, chunk // lanes, lanes)
        returned = lax.all_to_all(outgoing, "ctx", split_axis=0, concat_axis=0, tiled=True)
        mixed = (
            returned.reshape(cycle_size, local_rows, local_width)
            .transpose(1, 0, 2)
            .reshape(local_rows, model_width)
        )
        result = (wide_state + mixed.astype(jnp.float32)[None]).astype(jnp.bfloat16)
        if moment + 1 < moment_count:
            incoming = shifted(result, "pipe", 1)
        if moment >= phase_count - 1:
            finals.append(result)
    final_state = jnp.stack(finals, axis=0)
    last_phase = phase_count - 1
    is_last = phase_index == last_phase
    head_cols = head_weight.shape[1]
    final_norm = rms_scale(final_state.astype(jnp.float32), head_gain).astype(jnp.bfloat16)
    velocity_all = jnp.einsum(
        "mbsd,dp->mbsp", final_norm, head_full, preferred_element_type=jnp.float32
    )
    residue = velocity_all - target
    grad_all = jnp.einsum(
        "mbsd,mbsp->dp", final_norm.astype(jnp.float32), residue, precision=lax.Precision.HIGHEST
    ) / float(seq_total)
    grad_rows = lax.psum_scatter(grad_all, "dp", scatter_dimension=0, tiled=True)
    grad_rows = lax.psum(grad_rows, "ctx")
    velocity_in = jnp.zeros(velocity_all.shape[:3] + (head_cols,), jnp.float32)
    gradient_in = jnp.zeros((grad_rows.shape[0], head_cols), jnp.float32)
    for target_phase in range(last_phase):
        cols = slice(target_phase * head_cols, (target_phase + 1) * head_cols)
        pair = [(last_phase, target_phase)]
        velocity_in = velocity_in + lax.ppermute(velocity_all[..., cols], "pipe", pair)
        gradient_in = gradient_in + lax.ppermute(grad_rows[:, cols], "pipe", pair)
    own_cols = slice(last_phase * head_cols, phase_count * head_cols)
    velocity = jnp.where(is_last, velocity_all[..., own_cols], velocity_in)
    gradient = jnp.where(is_last, grad_rows[:, own_cols], gradient_in)
    return (velocity, gradient)


def solution(mesh):
    placed = (
        P(None, "dp", "ctx", None),
        P(None, "dp", "ctx", None),
        P(None, "dp"),
        P(None, "dp", None),
        P(),
        P(),
        P("pipe", "dp", None),
        P("pipe", "dp", None),
        P("pipe", None),
        P(),
        P(None, "pipe"),
    )
    return jax.shard_map(
        on_device,
        mesh=mesh,
        in_specs=placed,
        out_specs=(P(None, "dp", "ctx", "pipe"), P("dp", "pipe")),
        check_vma=False,
    )
```

```python
import jax
import jax.numpy as jnp
from jax import lax
from jax.sharding import PartitionSpec as P

HEAD = 96


epsilon = 1e-06


def shifted(value, axis, steps):
    count = lax.axis_size(axis)
    first, last = (max(0, -steps), min(count, count - steps))
    return lax.ppermute(value, axis, [(source, source + steps) for source in range(first, last)])


def rms_scale(values, gain_row):
    return (
        values * lax.rsqrt(jnp.mean(values * values, axis=-1, keepdims=True) + epsilon) * gain_row
    )


def on_device(
    clean_latent,
    noise_latent,
    time_index,
    frame_ids,
    embed_weight,
    time_vector,
    query_weight,
    key_weight,
    norm_gain,
    head_gain,
    head_weight,
):
    phase_index = lax.axis_index("pipe")
    phase_count = lax.axis_size("pipe")
    cycle_size = lax.axis_size("ctx")
    micro_count = clean_latent.shape[0]
    local_rows = clean_latent.shape[2]
    model_width = embed_weight.shape[1]
    head_count = model_width // HEAD
    local_heads = head_count // cycle_size
    local_width = local_heads * HEAD
    seq_total = local_rows * cycle_size
    score_scale = HEAD ** (-0.5)
    flow_time = ((time_index.astype(jnp.float32) + 0.5) / 1000.0)[:, :, None, None]
    noisy_input = ((1.0 - flow_time) * noise_latent + flow_time * clean_latent).astype(jnp.bfloat16)
    target = clean_latent - noise_latent
    embedded = jnp.einsum(
        "mbsp,pd->mbsd", noisy_input, embed_weight, preferred_element_type=jnp.float32
    )
    embedded = (embedded + flow_time * time_vector).astype(jnp.bfloat16)
    dp_index = lax.axis_index("dp")
    dp_count = lax.axis_size("dp")
    full_query = lax.all_gather(query_weight[0], "dp", axis=0, tiled=True)
    key_blocks = [key_weight[0]]
    for step in range(1, dp_count):
        pairs = [(source, (source + step) % dp_count) for source in range(dp_count)]
        key_blocks.append(lax.ppermute(key_weight[0], "dp", pairs))
    by_step = jnp.stack(key_blocks, axis=0)
    source_step = (dp_index - jnp.arange(dp_count, dtype=jnp.int32)) % dp_count
    full_key = jnp.take(by_step, source_step, axis=0).reshape(model_width, model_width)
    head_full = lax.all_gather(head_weight, "pipe", axis=1, tiled=True)
    full_query, full_key, head_full = lax.optimization_barrier((full_query, full_key, head_full))
    section_gain = norm_gain[0]

    def attention(by_heads, frame_row):
        query_all = by_heads[0].reshape(seq_total, local_heads, HEAD)
        key_all = by_heads[1].reshape(seq_total, local_heads, HEAD)
        value_all = by_heads[2].reshape(seq_total, local_heads, HEAD)
        allowed = frame_row[None, :] <= frame_row[:, None]
        scores = (
            jnp.einsum("shd,khd->hsk", query_all, key_all, preferred_element_type=jnp.float32)
            * score_scale
        )
        scores = jnp.where(allowed[None], scores, -1e30)
        row_max = jnp.max(scores, axis=-1, keepdims=True)
        weights = jnp.where(allowed[None], jnp.exp(scores - row_max), 0.0)
        row_sum = jnp.sum(weights, axis=-1)
        mixed = jnp.einsum(
            "hsk,khd->hsd",
            weights.astype(jnp.bfloat16),
            value_all,
            preferred_element_type=jnp.float32,
        ) / row_sum[..., None]
        return mixed.transpose(1, 0, 2).reshape(seq_total, local_width).astype(jnp.bfloat16)

    incoming = jnp.zeros((1, local_rows, model_width), jnp.bfloat16)
    finals = []
    moment_count = micro_count + phase_count - 1
    for moment in range(moment_count):
        micro_slot = jnp.clip(moment - phase_index, 0, micro_count - 1)
        active = jnp.logical_and(moment >= phase_index, moment - phase_index < micro_count)
        current = jnp.where(phase_index == 0, embedded[min(moment, micro_count - 1)], incoming)
        frame_row = lax.dynamic_index_in_dim(frame_ids, micro_slot, 0, keepdims=False)[0]
        wide_state = current.astype(jnp.float32)
        normed = rms_scale(wide_state, section_gain).astype(jnp.bfloat16)[0]

        def project(source):
            queries = jnp.dot(source, full_query, preferred_element_type=jnp.float32).astype(
                jnp.bfloat16
            )
            keys = jnp.dot(source, full_key, preferred_element_type=jnp.float32).astype(
                jnp.bfloat16
            )
            return jnp.stack((queries, keys, source), axis=0)

        def blank_triple(source):
            return jnp.zeros((3,) + source.shape, jnp.bfloat16)

        triple = lax.cond(active, project, blank_triple, normed)
        section_by_heads = lax.all_to_all(triple, "ctx", split_axis=2, concat_axis=1, tiled=True)

        def run_attention(arrived):
            return attention(arrived, frame_row)

        def blank_heads(arrived):
            return jnp.zeros((seq_total, local_width), jnp.bfloat16)

        mixed_heads = lax.cond(active, run_attention, blank_heads, section_by_heads)
        chunk = local_rows * local_width
        lanes = 128 if chunk % 128 == 0 else chunk
        outgoing = mixed_heads.reshape(cycle_size, chunk // lanes, lanes)
        returned = lax.all_to_all(outgoing, "ctx", split_axis=0, concat_axis=0, tiled=True)
        mixed = (
            returned.reshape(cycle_size, local_rows, local_width)
            .transpose(1, 0, 2)
            .reshape(local_rows, model_width)
        )
        result = (wide_state + mixed.astype(jnp.float32)[None]).astype(jnp.bfloat16)
        if moment + 1 < moment_count:
            incoming = shifted(result, "pipe", 1)
        if moment >= phase_count - 1:
            finals.append(result)
    final_state = jnp.stack(finals, axis=0)
    last_phase = phase_count - 1
    is_last = phase_index == last_phase
    head_cols = head_weight.shape[1]
    final_norm = rms_scale(final_state.astype(jnp.float32), head_gain).astype(jnp.bfloat16)
    velocity_all = jnp.einsum(
        "mbsd,dp->mbsp", final_norm, head_full, preferred_element_type=jnp.float32
    )
    residue = velocity_all - target
    grad_all = jnp.einsum(
        "mbsd,mbsp->dp", final_norm.astype(jnp.float32), residue, precision=lax.Precision.HIGHEST
    ) / float(seq_total)
    grad_rows = lax.psum_scatter(grad_all, "dp", scatter_dimension=0, tiled=True)
    grad_rows = lax.psum(grad_rows, "ctx")
    velocity_in = jnp.zeros(velocity_all.shape[:3] + (head_cols,), jnp.float32)
    gradient_in = jnp.zeros((grad_rows.shape[0], head_cols), jnp.float32)
    for target_phase in range(last_phase):
        cols = slice(target_phase * head_cols, (target_phase + 1) * head_cols)
        pair = [(last_phase, target_phase)]
        velocity_in = velocity_in + lax.ppermute(velocity_all[..., cols], "pipe", pair)
        gradient_in = gradient_in + lax.ppermute(grad_rows[:, cols], "pipe", pair)
    own_cols = slice(last_phase * head_cols, phase_count * head_cols)
    velocity = jnp.where(is_last, velocity_all[..., own_cols], velocity_in)
    gradient = jnp.where(is_last, grad_rows[:, own_cols], gradient_in)
    return (velocity, gradient)


def solution(mesh):
    placed = (
        P(None, "dp", "ctx", None),
        P(None, "dp", "ctx", None),
        P(None, "dp"),
        P(None, "dp", None),
        P(),
        P(),
        P("pipe", "dp", None),
        P("pipe", "dp", None),
        P("pipe", None),
        P(),
        P(None, "pipe"),
    )
    return jax.shard_map(
        on_device,
        mesh=mesh,
        in_specs=placed,
        out_specs=(P(None, "dp", "ctx", "pipe"), P("dp", "pipe")),
        check_vma=False,
    )
```

```python
import jax
import jax.numpy as jnp
from jax import lax
from jax.sharding import PartitionSpec as P

HEAD = 96


epsilon = 1e-06


def shifted(value, axis, steps):
    count = lax.axis_size(axis)
    first, last = (max(0, -steps), min(count, count - steps))
    return lax.ppermute(value, axis, [(source, source + steps) for source in range(first, last)])


def rms_scale(values, gain_row):
    return (
        values * lax.rsqrt(jnp.mean(values * values, axis=-1, keepdims=True) + epsilon) * gain_row
    )


def on_device(
    clean_latent,
    noise_latent,
    time_index,
    frame_ids,
    embed_weight,
    time_vector,
    query_weight,
    key_weight,
    norm_gain,
    head_gain,
    head_weight,
):
    phase_index = lax.axis_index("pipe")
    phase_count = lax.axis_size("pipe")
    cycle_size = lax.axis_size("ctx")
    micro_count = clean_latent.shape[0]
    local_rows = clean_latent.shape[2]
    model_width = embed_weight.shape[1]
    head_count = model_width // HEAD
    local_heads = head_count // cycle_size
    local_width = local_heads * HEAD
    seq_total = local_rows * cycle_size
    score_scale = HEAD ** (-0.5)
    flow_time = ((time_index.astype(jnp.float32) + 0.5) / 1000.0)[:, :, None, None]
    noisy_input = ((1.0 - flow_time) * noise_latent + flow_time * clean_latent).astype(jnp.bfloat16)
    target = clean_latent - noise_latent
    embedded = jnp.einsum(
        "mbsp,pd->mbsd", noisy_input, embed_weight, preferred_element_type=jnp.float32
    )
    embedded = (embedded + flow_time * time_vector).astype(jnp.bfloat16)
    dp_index = lax.axis_index("dp")
    dp_count = lax.axis_size("dp")
    full_query = lax.all_gather(query_weight[0], "dp", axis=0, tiled=True)
    key_blocks = [key_weight[0]]
    for step in range(1, dp_count):
        pairs = [(source, (source + step) % dp_count) for source in range(dp_count)]
        key_blocks.append(lax.ppermute(key_weight[0], "dp", pairs))
    by_step = jnp.stack(key_blocks, axis=0)
    source_step = (dp_index - jnp.arange(dp_count, dtype=jnp.int32)) % dp_count
    full_key = jnp.take(by_step, source_step, axis=0).reshape(model_width, model_width)
    last_phase = phase_count - 1
    head_pieces = []
    for source_phase in range(phase_count):
        if source_phase == last_phase:
            head_pieces.append(head_weight)
        else:
            head_pieces.append(lax.ppermute(head_weight, "pipe", [(source_phase, last_phase)]))
    head_full = jnp.concatenate(head_pieces, axis=1)
    section_gain = norm_gain[0]

    def attention(by_heads, frame_row):
        query_all = by_heads[0].reshape(seq_total, local_heads, HEAD)
        key_all = by_heads[1].reshape(seq_total, local_heads, HEAD)
        value_all = by_heads[2].reshape(seq_total, local_heads, HEAD)
        allowed = frame_row[None, :] <= frame_row[:, None]
        scores = (
            jnp.einsum("shd,khd->hsk", query_all, key_all, preferred_element_type=jnp.float32)
            * score_scale
        )
        scores = jnp.where(allowed[None], scores, -1e30)
        row_max = jnp.max(scores, axis=-1, keepdims=True)
        weights = jnp.where(allowed[None], jnp.exp(scores - row_max), 0.0)
        row_sum = jnp.sum(weights, axis=-1)
        mixed = jnp.einsum(
            "hsk,khd->hsd",
            weights.astype(jnp.bfloat16),
            value_all,
            preferred_element_type=jnp.float32,
        ) / row_sum[..., None]
        return mixed.transpose(1, 0, 2).reshape(seq_total, local_width).astype(jnp.bfloat16)

    incoming = jnp.zeros((1, local_rows, model_width), jnp.bfloat16)
    finals = []
    moment_count = micro_count + phase_count - 1
    for moment in range(moment_count):
        micro_slot = jnp.clip(moment - phase_index, 0, micro_count - 1)
        active = jnp.logical_and(moment >= phase_index, moment - phase_index < micro_count)
        current = jnp.where(phase_index == 0, embedded[min(moment, micro_count - 1)], incoming)
        frame_row = lax.dynamic_index_in_dim(frame_ids, micro_slot, 0, keepdims=False)[0]
        wide_state = current.astype(jnp.float32)
        normed = rms_scale(wide_state, section_gain).astype(jnp.bfloat16)[0]

        def project(source):
            queries = jnp.dot(source, full_query, preferred_element_type=jnp.float32).astype(
                jnp.bfloat16
            )
            keys = jnp.dot(source, full_key, preferred_element_type=jnp.float32).astype(
                jnp.bfloat16
            )
            return jnp.stack((queries, keys, source), axis=0)

        def blank_triple(source):
            return jnp.zeros((3,) + source.shape, jnp.bfloat16)

        triple = lax.cond(active, project, blank_triple, normed)
        section_by_heads = lax.all_to_all(triple, "ctx", split_axis=2, concat_axis=1, tiled=True)

        def run_attention(arrived):
            return attention(arrived, frame_row)

        def blank_heads(arrived):
            return jnp.zeros((seq_total, local_width), jnp.bfloat16)

        mixed_heads = lax.cond(active, run_attention, blank_heads, section_by_heads)
        chunk = local_rows * local_width
        lanes = 128 if chunk % 128 == 0 else chunk
        outgoing = mixed_heads.reshape(cycle_size, chunk // lanes, lanes)
        returned = lax.all_to_all(outgoing, "ctx", split_axis=0, concat_axis=0, tiled=True)
        mixed = (
            returned.reshape(cycle_size, local_rows, local_width)
            .transpose(1, 0, 2)
            .reshape(local_rows, model_width)
        )
        result = (wide_state + mixed.astype(jnp.float32)[None]).astype(jnp.bfloat16)
        if moment + 1 < moment_count:
            incoming = shifted(result, "pipe", 1)
        if moment >= phase_count - 1:
            finals.append(result)
    final_state = jnp.stack(finals, axis=0)
    is_last = phase_index == last_phase
    head_cols = head_weight.shape[1]
    final_norm = rms_scale(final_state.astype(jnp.float32), head_gain).astype(jnp.bfloat16)
    velocity_all = jnp.einsum(
        "mbsd,dp->mbsp", final_norm, head_full, preferred_element_type=jnp.float32
    )
    residue = velocity_all - target
    grad_all = jnp.einsum(
        "mbsd,mbsp->dp", final_norm.astype(jnp.float32), residue, precision=lax.Precision.HIGHEST
    ) / float(seq_total)
    grad_rows = lax.psum_scatter(grad_all, "dp", scatter_dimension=0, tiled=True)
    grad_rows = lax.psum(grad_rows, "ctx")
    velocity_in = jnp.zeros(velocity_all.shape[:3] + (head_cols,), jnp.float32)
    gradient_in = jnp.zeros((grad_rows.shape[0], head_cols), jnp.float32)
    for target_phase in range(last_phase):
        cols = slice(target_phase * head_cols, (target_phase + 1) * head_cols)
        pair = [(last_phase, target_phase)]
        velocity_in = velocity_in + lax.ppermute(velocity_all[..., cols], "pipe", pair)
        gradient_in = gradient_in + lax.ppermute(grad_rows[:, cols], "pipe", pair)
    own_cols = slice(last_phase * head_cols, phase_count * head_cols)
    velocity = jnp.where(is_last, velocity_all[..., own_cols], velocity_in)
    gradient = jnp.where(is_last, grad_rows[:, own_cols], gradient_in)
    return (velocity, gradient)


def solution(mesh):
    placed = (
        P(None, "dp", "ctx", None),
        P(None, "dp", "ctx", None),
        P(None, "dp"),
        P(None, "dp", None),
        P(),
        P(),
        P("pipe", "dp", None),
        P("pipe", "dp", None),
        P("pipe", None),
        P(),
        P(None, "pipe"),
    )
    return jax.shard_map(
        on_device,
        mesh=mesh,
        in_specs=placed,
        out_specs=(P(None, "dp", "ctx", "pipe"), P("dp", "pipe")),
        check_vma=False,
    )
```

```python
import jax
import jax.numpy as jnp
from jax import lax
from jax.sharding import PartitionSpec as P

HEAD = 96


epsilon = 1e-06


def shifted(value, axis, steps):
    count = lax.axis_size(axis)
    first, last = (max(0, -steps), min(count, count - steps))
    return lax.ppermute(value, axis, [(source, source + steps) for source in range(first, last)])


def rms_scale(values, gain_row):
    return (
        values * lax.rsqrt(jnp.mean(values * values, axis=-1, keepdims=True) + epsilon) * gain_row
    )


def on_device(
    clean_latent,
    noise_latent,
    time_index,
    frame_ids,
    embed_weight,
    time_vector,
    query_weight,
    key_weight,
    norm_gain,
    head_gain,
    head_weight,
):
    phase_index = lax.axis_index("pipe")
    phase_count = lax.axis_size("pipe")
    cycle_size = lax.axis_size("ctx")
    micro_count = clean_latent.shape[0]
    local_rows = clean_latent.shape[2]
    model_width = embed_weight.shape[1]
    head_count = model_width // HEAD
    local_heads = head_count // cycle_size
    local_width = local_heads * HEAD
    seq_total = local_rows * cycle_size
    score_scale = HEAD ** (-0.5)
    flow_time = ((time_index.astype(jnp.float32) + 0.5) / 1000.0)[:, :, None, None]
    noisy_input = ((1.0 - flow_time) * noise_latent + flow_time * clean_latent).astype(jnp.bfloat16)
    target = clean_latent - noise_latent
    embedded = jnp.einsum(
        "mbsp,pd->mbsd", noisy_input, embed_weight, preferred_element_type=jnp.float32
    )
    embedded = (embedded + flow_time * time_vector).astype(jnp.bfloat16)
    dp_index = lax.axis_index("dp")
    dp_count = lax.axis_size("dp")
    full_query = lax.all_gather(query_weight[0], "dp", axis=0, tiled=True)
    key_blocks = [key_weight[0]]
    for step in range(1, dp_count):
        pairs = [(source, (source + step) % dp_count) for source in range(dp_count)]
        key_blocks.append(lax.ppermute(key_weight[0], "dp", pairs))
    by_step = jnp.stack(key_blocks, axis=0)
    source_step = (dp_index - jnp.arange(dp_count, dtype=jnp.int32)) % dp_count
    full_key = jnp.take(by_step, source_step, axis=0).reshape(model_width, model_width)
    last_phase = phase_count - 1
    head_pieces = []
    for source_phase in range(phase_count):
        if source_phase == last_phase:
            head_pieces.append(head_weight)
        else:
            head_pieces.append(lax.ppermute(head_weight, "pipe", [(source_phase, last_phase)]))
    head_full = jnp.concatenate(head_pieces, axis=1)
    section_gain = norm_gain[0]

    def attention(by_heads, frame_row):
        query_all = by_heads[0].reshape(seq_total, local_heads, HEAD)
        key_all = by_heads[1].reshape(seq_total, local_heads, HEAD)
        value_all = by_heads[2].reshape(seq_total, local_heads, HEAD)
        allowed = frame_row[None, :] <= frame_row[:, None]
        scores = (
            jnp.einsum("shd,khd->hsk", query_all, key_all, preferred_element_type=jnp.float32)
            * score_scale
        )
        scores = jnp.where(allowed[None], scores, -1e30)
        row_max = jnp.max(scores, axis=-1, keepdims=True)
        weights = jnp.where(allowed[None], jnp.exp(scores - row_max), 0.0)
        row_sum = jnp.sum(weights, axis=-1)
        mixed = jnp.einsum(
            "hsk,khd->hsd",
            weights.astype(jnp.bfloat16),
            value_all,
            preferred_element_type=jnp.float32,
        ) / row_sum[..., None]
        return mixed.transpose(1, 0, 2).reshape(seq_total, local_width).astype(jnp.bfloat16)

    incoming = jnp.zeros((1, local_rows, model_width), jnp.bfloat16)
    finals = []
    moment_count = micro_count + phase_count - 1
    for moment in range(moment_count):
        micro_slot = jnp.clip(moment - phase_index, 0, micro_count - 1)
        active = jnp.logical_and(moment >= phase_index, moment - phase_index < micro_count)
        current = jnp.where(phase_index == 0, embedded[min(moment, micro_count - 1)], incoming)
        frame_row = lax.dynamic_index_in_dim(frame_ids, micro_slot, 0, keepdims=False)[0]
        wide_state = current.astype(jnp.float32)
        normed = rms_scale(wide_state, section_gain).astype(jnp.bfloat16)[0]

        def project(source):
            queries = jnp.dot(source, full_query, preferred_element_type=jnp.float32).astype(
                jnp.bfloat16
            )
            keys = jnp.dot(source, full_key, preferred_element_type=jnp.float32).astype(
                jnp.bfloat16
            )
            return jnp.stack((queries, keys, source), axis=0)

        def blank_triple(source):
            return jnp.zeros((3,) + source.shape, jnp.bfloat16)

        triple = lax.cond(active, project, blank_triple, normed)
        section_by_heads = lax.all_to_all(triple, "ctx", split_axis=2, concat_axis=1, tiled=True)

        def run_attention(arrived):
            return attention(arrived, frame_row)

        def blank_heads(arrived):
            return jnp.zeros((seq_total, local_width), jnp.bfloat16)

        mixed_heads = lax.cond(active, run_attention, blank_heads, section_by_heads)
        chunk = local_rows * local_width
        lanes = 128 if chunk % 128 == 0 else chunk
        outgoing = mixed_heads.reshape(cycle_size, chunk // lanes, lanes)
        returned = lax.all_to_all(outgoing, "ctx", split_axis=0, concat_axis=0, tiled=True)
        mixed = (
            returned.reshape(cycle_size, local_rows, local_width)
            .transpose(1, 0, 2)
            .reshape(local_rows, model_width)
        )
        result = (wide_state + mixed.astype(jnp.float32)[None]).astype(jnp.bfloat16)
        if moment + 1 < moment_count:
            incoming = shifted(result, "pipe", 1)
        if moment >= phase_count - 1:
            finals.append(result)
    final_state = jnp.stack(finals, axis=0)
    is_last = phase_index == last_phase
    head_cols = head_weight.shape[1]
    final_norm = rms_scale(final_state.astype(jnp.float32), head_gain).astype(jnp.bfloat16)
    velocity_all = jnp.einsum(
        "mbsd,dp->mbsp", final_norm, head_full, preferred_element_type=jnp.float32
    )
    residue = velocity_all - target
    grad_all = jnp.einsum(
        "mbsd,mbsp->dp", final_norm.astype(jnp.float32), residue, precision=lax.Precision.HIGHEST
    ) / float(seq_total)
    grad_rows = lax.psum_scatter(grad_all, "dp", scatter_dimension=0, tiled=True)
    grad_rows = lax.psum(grad_rows, "ctx")
    velocity_shape = velocity_all.shape[:3] + (head_cols,)
    velocity_size = velocity_all.size // phase_count
    gradient_shape = (grad_rows.shape[0], head_cols)
    packed_in = jnp.zeros((velocity_size + grad_rows.size // phase_count,), jnp.float32)
    for target_phase in range(last_phase):
        cols = slice(target_phase * head_cols, (target_phase + 1) * head_cols)
        packed = jnp.concatenate(
            (velocity_all[..., cols].reshape(-1), grad_rows[:, cols].reshape(-1))
        )
        packed_in = packed_in + lax.ppermute(packed, "pipe", [(last_phase, target_phase)])
    own_cols = slice(last_phase * head_cols, phase_count * head_cols)
    velocity_in = packed_in[:velocity_size].reshape(velocity_shape)
    gradient_in = packed_in[velocity_size:].reshape(gradient_shape)
    velocity = jnp.where(is_last, velocity_all[..., own_cols], velocity_in)
    gradient = jnp.where(is_last, grad_rows[:, own_cols], gradient_in)
    return (velocity, gradient)


def solution(mesh):
    placed = (
        P(None, "dp", "ctx", None),
        P(None, "dp", "ctx", None),
        P(None, "dp"),
        P(None, "dp", None),
        P(),
        P(),
        P("pipe", "dp", None),
        P("pipe", "dp", None),
        P("pipe", None),
        P(),
        P(None, "pipe"),
    )
    return jax.shard_map(
        on_device,
        mesh=mesh,
        in_specs=placed,
        out_specs=(P(None, "dp", "ctx", "pipe"), P("dp", "pipe")),
        check_vma=False,
    )
```

```python
import jax
import jax.numpy as jnp
from jax import lax
from jax.sharding import PartitionSpec as P

HEAD = 96


epsilon = 1e-06


def shifted(value, axis, steps):
    count = lax.axis_size(axis)
    first, last = (max(0, -steps), min(count, count - steps))
    return lax.ppermute(value, axis, [(source, source + steps) for source in range(first, last)])


def rms_scale(values, gain_row):
    return (
        values * lax.rsqrt(jnp.mean(values * values, axis=-1, keepdims=True) + epsilon) * gain_row
    )


def on_device(
    clean_latent,
    noise_latent,
    time_index,
    frame_ids,
    embed_weight,
    time_vector,
    query_weight,
    key_weight,
    norm_gain,
    head_gain,
    head_weight,
):
    phase_index = lax.axis_index("pipe")
    phase_count = lax.axis_size("pipe")
    cycle_size = lax.axis_size("ctx")
    micro_count = clean_latent.shape[0]
    local_rows = clean_latent.shape[2]
    model_width = embed_weight.shape[1]
    head_count = model_width // HEAD
    local_heads = head_count // cycle_size
    local_width = local_heads * HEAD
    seq_total = local_rows * cycle_size
    score_scale = HEAD ** (-0.5)
    flow_time = ((time_index.astype(jnp.float32) + 0.5) / 1000.0)[:, :, None, None]
    noisy_input = ((1.0 - flow_time) * noise_latent + flow_time * clean_latent).astype(jnp.bfloat16)
    target = clean_latent - noise_latent
    embedded = jnp.einsum(
        "mbsp,pd->mbsd", noisy_input, embed_weight, preferred_element_type=jnp.float32
    )
    embedded = (embedded + flow_time * time_vector).astype(jnp.bfloat16)
    dp_index = lax.axis_index("dp")
    dp_count = lax.axis_size("dp")
    full_query = lax.all_gather(query_weight[0], "dp", axis=0, tiled=True)
    key_blocks = [key_weight[0]]
    for step in range(1, dp_count):
        pairs = [(source, (source + step) % dp_count) for source in range(dp_count)]
        key_blocks.append(lax.ppermute(key_weight[0], "dp", pairs))
    by_step = jnp.stack(key_blocks, axis=0)
    source_step = (dp_index - jnp.arange(dp_count, dtype=jnp.int32)) % dp_count
    full_key = jnp.take(by_step, source_step, axis=0).reshape(model_width, model_width)
    last_phase = phase_count - 1
    head_pieces = []
    for source_phase in range(phase_count):
        if source_phase == last_phase:
            head_pieces.append(head_weight)
        else:
            head_pieces.append(lax.ppermute(head_weight, "pipe", [(source_phase, last_phase)]))
    head_full = jnp.concatenate(head_pieces, axis=1)
    full_query, full_key, head_full = lax.optimization_barrier((full_query, full_key, head_full))
    section_gain = norm_gain[0]

    def attention(by_heads, frame_row):
        query_all = by_heads[0].reshape(seq_total, local_heads, HEAD)
        key_all = by_heads[1].reshape(seq_total, local_heads, HEAD)
        value_all = by_heads[2].reshape(seq_total, local_heads, HEAD)
        allowed = frame_row[None, :] <= frame_row[:, None]
        scores = (
            jnp.einsum("shd,khd->hsk", query_all, key_all, preferred_element_type=jnp.float32)
            * score_scale
        )
        scores = jnp.where(allowed[None], scores, -1e30)
        row_max = jnp.max(scores, axis=-1, keepdims=True)
        weights = jnp.where(allowed[None], jnp.exp(scores - row_max), 0.0)
        row_sum = jnp.sum(weights, axis=-1)
        mixed = jnp.einsum(
            "hsk,khd->hsd",
            weights.astype(jnp.bfloat16),
            value_all,
            preferred_element_type=jnp.float32,
        ) / row_sum[..., None]
        return mixed.transpose(1, 0, 2).reshape(seq_total, local_width).astype(jnp.bfloat16)

    incoming = jnp.zeros((1, local_rows, model_width), jnp.bfloat16)
    finals = []
    moment_count = micro_count + phase_count - 1
    for moment in range(moment_count):
        micro_slot = jnp.clip(moment - phase_index, 0, micro_count - 1)
        active = jnp.logical_and(moment >= phase_index, moment - phase_index < micro_count)
        current = jnp.where(phase_index == 0, embedded[min(moment, micro_count - 1)], incoming)
        frame_row = lax.dynamic_index_in_dim(frame_ids, micro_slot, 0, keepdims=False)[0]
        wide_state = current.astype(jnp.float32)
        normed = rms_scale(wide_state, section_gain).astype(jnp.bfloat16)[0]

        def project(source):
            queries = jnp.dot(source, full_query, preferred_element_type=jnp.float32).astype(
                jnp.bfloat16
            )
            keys = jnp.dot(source, full_key, preferred_element_type=jnp.float32).astype(
                jnp.bfloat16
            )
            return jnp.stack((queries, keys, source), axis=0)

        def blank_triple(source):
            return jnp.zeros((3,) + source.shape, jnp.bfloat16)

        triple = lax.cond(active, project, blank_triple, normed)
        section_by_heads = lax.all_to_all(triple, "ctx", split_axis=2, concat_axis=1, tiled=True)

        def run_attention(arrived):
            return attention(arrived, frame_row)

        def blank_heads(arrived):
            return jnp.zeros((seq_total, local_width), jnp.bfloat16)

        mixed_heads = lax.cond(active, run_attention, blank_heads, section_by_heads)
        chunk = local_rows * local_width
        lanes = 128 if chunk % 128 == 0 else chunk
        outgoing = mixed_heads.reshape(cycle_size, chunk // lanes, lanes)
        returned = lax.all_to_all(outgoing, "ctx", split_axis=0, concat_axis=0, tiled=True)
        mixed = (
            returned.reshape(cycle_size, local_rows, local_width)
            .transpose(1, 0, 2)
            .reshape(local_rows, model_width)
        )
        result = (wide_state + mixed.astype(jnp.float32)[None]).astype(jnp.bfloat16)
        if moment + 1 < moment_count:
            incoming = shifted(result, "pipe", 1)
        if moment >= phase_count - 1:
            finals.append(result)
    final_state = jnp.stack(finals, axis=0)
    is_last = phase_index == last_phase
    head_cols = head_weight.shape[1]
    final_norm = rms_scale(final_state.astype(jnp.float32), head_gain).astype(jnp.bfloat16)
    velocity_all = jnp.einsum(
        "mbsd,dp->mbsp", final_norm, head_full, preferred_element_type=jnp.float32
    )
    residue = velocity_all - target
    grad_all = jnp.einsum(
        "mbsd,mbsp->dp", final_norm.astype(jnp.float32), residue, precision=lax.Precision.HIGHEST
    ) / float(seq_total)
    grad_rows = lax.psum_scatter(grad_all, "dp", scatter_dimension=0, tiled=True)
    grad_rows = lax.psum(grad_rows, "ctx")
    velocity_shape = velocity_all.shape[:3] + (head_cols,)
    velocity_size = velocity_all.size // phase_count
    gradient_shape = (grad_rows.shape[0], head_cols)
    packed_in = jnp.zeros((velocity_size + grad_rows.size // phase_count,), jnp.float32)
    for target_phase in range(last_phase):
        cols = slice(target_phase * head_cols, (target_phase + 1) * head_cols)
        packed = jnp.concatenate(
            (velocity_all[..., cols].reshape(-1), grad_rows[:, cols].reshape(-1))
        )
        packed_in = packed_in + lax.ppermute(packed, "pipe", [(last_phase, target_phase)])
    own_cols = slice(last_phase * head_cols, phase_count * head_cols)
    velocity_in = packed_in[:velocity_size].reshape(velocity_shape)
    gradient_in = packed_in[velocity_size:].reshape(gradient_shape)
    velocity = jnp.where(is_last, velocity_all[..., own_cols], velocity_in)
    gradient = jnp.where(is_last, grad_rows[:, own_cols], gradient_in)
    return (velocity, gradient)


def solution(mesh):
    placed = (
        P(None, "dp", "ctx", None),
        P(None, "dp", "ctx", None),
        P(None, "dp"),
        P(None, "dp", None),
        P(),
        P(),
        P("pipe", "dp", None),
        P("pipe", "dp", None),
        P("pipe", None),
        P(),
        P(None, "pipe"),
    )
    return jax.shard_map(
        on_device,
        mesh=mesh,
        in_specs=placed,
        out_specs=(P(None, "dp", "ctx", "pipe"), P("dp", "pipe")),
        check_vma=False,
    )
```

```python
import jax
import jax.numpy as jnp
from jax import lax
from jax.sharding import PartitionSpec as P

HEAD = 96


epsilon = 1e-06


def shifted(value, axis, steps):
    count = lax.axis_size(axis)
    first, last = (max(0, -steps), min(count, count - steps))
    return lax.ppermute(value, axis, [(source, source + steps) for source in range(first, last)])


def rms_scale(values, gain_row):
    return (
        values * lax.rsqrt(jnp.mean(values * values, axis=-1, keepdims=True) + epsilon) * gain_row
    )


def on_device(
    clean_latent,
    noise_latent,
    time_index,
    frame_ids,
    embed_weight,
    time_vector,
    query_weight,
    key_weight,
    norm_gain,
    head_gain,
    head_weight,
):
    phase_index = lax.axis_index("pipe")
    phase_count = lax.axis_size("pipe")
    cycle_size = lax.axis_size("ctx")
    micro_count = clean_latent.shape[0]
    local_rows = clean_latent.shape[2]
    model_width = embed_weight.shape[1]
    head_count = model_width // HEAD
    local_heads = head_count // cycle_size
    local_width = local_heads * HEAD
    seq_total = local_rows * cycle_size
    score_scale = HEAD ** (-0.5)
    flow_time = ((time_index.astype(jnp.float32) + 0.5) / 1000.0)[:, :, None, None]
    noisy_input = ((1.0 - flow_time) * noise_latent + flow_time * clean_latent).astype(jnp.bfloat16)
    target = clean_latent - noise_latent
    embedded = jnp.einsum(
        "mbsp,pd->mbsd", noisy_input, embed_weight, preferred_element_type=jnp.float32
    )
    embedded = (embedded + flow_time * time_vector).astype(jnp.bfloat16)
    dp_index = lax.axis_index("dp")
    dp_count = lax.axis_size("dp")
    full_query = lax.all_gather(query_weight[0], "dp", axis=0, tiled=True)
    key_blocks = [key_weight[0]]
    for step in range(1, dp_count):
        pairs = [(source, (source + step) % dp_count) for source in range(dp_count)]
        key_blocks.append(lax.ppermute(key_weight[0], "dp", pairs))
    by_step = jnp.stack(key_blocks, axis=0)
    source_step = (dp_index - jnp.arange(dp_count, dtype=jnp.int32)) % dp_count
    full_key = jnp.take(by_step, source_step, axis=0).reshape(model_width, model_width)
    last_phase = phase_count - 1
    head_pieces = []
    for source_phase in range(phase_count):
        if source_phase == last_phase:
            head_pieces.append(head_weight)
        else:
            head_pieces.append(lax.ppermute(head_weight, "pipe", [(source_phase, last_phase)]))
    head_full = jnp.concatenate(head_pieces, axis=1)
    section_gain = norm_gain[0]

    def attention(by_heads, frame_row):
        query_all = by_heads[0].reshape(seq_total, local_heads, HEAD)
        key_all = by_heads[1].reshape(seq_total, local_heads, HEAD)
        value_all = by_heads[2].reshape(seq_total, local_heads, HEAD)
        allowed = frame_row[None, :] <= frame_row[:, None]
        scores = (
            jnp.einsum("shd,khd->hsk", query_all, key_all, preferred_element_type=jnp.float32)
            * score_scale
        )
        scores = jnp.where(allowed[None], scores, -1e30)
        row_max = jnp.max(scores, axis=-1, keepdims=True)
        weights = jnp.where(allowed[None], jnp.exp(scores - row_max), 0.0)
        row_sum = jnp.sum(weights, axis=-1)
        mixed = jnp.einsum(
            "hsk,khd->hsd",
            weights.astype(jnp.bfloat16),
            value_all,
            preferred_element_type=jnp.float32,
        ) / row_sum[..., None]
        return mixed.transpose(1, 0, 2).reshape(seq_total, local_width).astype(jnp.bfloat16)

    incoming = jnp.zeros((1, local_rows, model_width), jnp.bfloat16)
    finals = []
    moment_count = micro_count + phase_count - 1
    for moment in range(moment_count):
        micro_slot = jnp.clip(moment - phase_index, 0, micro_count - 1)
        active = jnp.logical_and(moment >= phase_index, moment - phase_index < micro_count)
        current = jnp.where(phase_index == 0, embedded[min(moment, micro_count - 1)], incoming)
        frame_row = lax.dynamic_index_in_dim(frame_ids, micro_slot, 0, keepdims=False)[0]
        wide_state = current.astype(jnp.float32)
        normed = rms_scale(wide_state, section_gain).astype(jnp.bfloat16)[0]

        def project(source):
            queries = jnp.dot(source, full_query, preferred_element_type=jnp.float32).astype(
                jnp.bfloat16
            )
            keys = jnp.dot(source, full_key, preferred_element_type=jnp.float32).astype(
                jnp.bfloat16
            )
            return jnp.stack((queries, keys, source), axis=0)

        def blank_triple(source):
            return jnp.zeros((3,) + source.shape, jnp.bfloat16)

        if moment == 0:
            value_heads = lax.all_to_all(
                normed[None], "ctx", split_axis=2, concat_axis=1, tiled=True
            )
            pair = lax.cond(active, project, blank_triple, normed)[:2]
            pair_heads = lax.all_to_all(pair, "ctx", split_axis=2, concat_axis=1, tiled=True)
            section_by_heads = jnp.concatenate((pair_heads, value_heads), axis=0)
        else:
            triple = lax.cond(active, project, blank_triple, normed)
            section_by_heads = lax.all_to_all(
                triple, "ctx", split_axis=2, concat_axis=1, tiled=True
            )

        def run_attention(arrived):
            return attention(arrived, frame_row)

        def blank_heads(arrived):
            return jnp.zeros((seq_total, local_width), jnp.bfloat16)

        mixed_heads = lax.cond(active, run_attention, blank_heads, section_by_heads)
        chunk = local_rows * local_width
        lanes = 128 if chunk % 128 == 0 else chunk
        outgoing = mixed_heads.reshape(cycle_size, chunk // lanes, lanes)
        returned = lax.all_to_all(outgoing, "ctx", split_axis=0, concat_axis=0, tiled=True)
        mixed = (
            returned.reshape(cycle_size, local_rows, local_width)
            .transpose(1, 0, 2)
            .reshape(local_rows, model_width)
        )
        result = (wide_state + mixed.astype(jnp.float32)[None]).astype(jnp.bfloat16)
        if moment + 1 < moment_count:
            incoming = shifted(result, "pipe", 1)
        if moment >= phase_count - 1:
            finals.append(result)
    final_state = jnp.stack(finals, axis=0)
    is_last = phase_index == last_phase
    head_cols = head_weight.shape[1]
    final_norm = rms_scale(final_state.astype(jnp.float32), head_gain).astype(jnp.bfloat16)
    velocity_all = jnp.einsum(
        "mbsd,dp->mbsp", final_norm, head_full, preferred_element_type=jnp.float32
    )
    residue = velocity_all - target
    grad_all = jnp.einsum(
        "mbsd,mbsp->dp", final_norm.astype(jnp.float32), residue, precision=lax.Precision.HIGHEST
    ) / float(seq_total)
    grad_rows = lax.psum_scatter(grad_all, "dp", scatter_dimension=0, tiled=True)
    grad_rows = lax.psum(grad_rows, "ctx")
    velocity_in = jnp.zeros(velocity_all.shape[:3] + (head_cols,), jnp.float32)
    gradient_in = jnp.zeros((grad_rows.shape[0], head_cols), jnp.float32)
    for target_phase in range(last_phase):
        cols = slice(target_phase * head_cols, (target_phase + 1) * head_cols)
        pair = [(last_phase, target_phase)]
        velocity_in = velocity_in + lax.ppermute(velocity_all[..., cols], "pipe", pair)
        gradient_in = gradient_in + lax.ppermute(grad_rows[:, cols], "pipe", pair)
    own_cols = slice(last_phase * head_cols, phase_count * head_cols)
    velocity = jnp.where(is_last, velocity_all[..., own_cols], velocity_in)
    gradient = jnp.where(is_last, grad_rows[:, own_cols], gradient_in)
    return (velocity, gradient)


def solution(mesh):
    placed = (
        P(None, "dp", "ctx", None),
        P(None, "dp", "ctx", None),
        P(None, "dp"),
        P(None, "dp", None),
        P(),
        P(),
        P("pipe", "dp", None),
        P("pipe", "dp", None),
        P("pipe", None),
        P(),
        P(None, "pipe"),
    )
    return jax.shard_map(
        on_device,
        mesh=mesh,
        in_specs=placed,
        out_specs=(P(None, "dp", "ctx", "pipe"), P("dp", "pipe")),
        check_vma=False,
    )
```

```python
import jax
import jax.numpy as jnp
from jax import lax
from jax.sharding import PartitionSpec as P

HEAD = 96


epsilon = 1e-06


def shifted(value, axis, steps):
    count = lax.axis_size(axis)
    first, last = (max(0, -steps), min(count, count - steps))
    return lax.ppermute(value, axis, [(source, source + steps) for source in range(first, last)])


def rms_scale(values, gain_row):
    return (
        values * lax.rsqrt(jnp.mean(values * values, axis=-1, keepdims=True) + epsilon) * gain_row
    )


def on_device(
    clean_latent,
    noise_latent,
    time_index,
    frame_ids,
    embed_weight,
    time_vector,
    query_weight,
    key_weight,
    norm_gain,
    head_gain,
    head_weight,
):
    phase_index = lax.axis_index("pipe")
    phase_count = lax.axis_size("pipe")
    cycle_size = lax.axis_size("ctx")
    micro_count = clean_latent.shape[0]
    local_rows = clean_latent.shape[2]
    model_width = embed_weight.shape[1]
    head_count = model_width // HEAD
    local_heads = head_count // cycle_size
    local_width = local_heads * HEAD
    seq_total = local_rows * cycle_size
    score_scale = HEAD ** (-0.5)
    flow_time = ((time_index.astype(jnp.float32) + 0.5) / 1000.0)[:, :, None, None]
    noisy_input = ((1.0 - flow_time) * noise_latent + flow_time * clean_latent).astype(jnp.bfloat16)
    target = clean_latent - noise_latent
    embedded = jnp.einsum(
        "mbsp,pd->mbsd", noisy_input, embed_weight, preferred_element_type=jnp.float32
    )
    embedded = (embedded + flow_time * time_vector).astype(jnp.bfloat16)
    dp_index = lax.axis_index("dp")
    dp_count = lax.axis_size("dp")
    full_query = lax.all_gather(query_weight[0], "dp", axis=0, tiled=True)
    key_blocks = [key_weight[0]]
    for step in range(1, dp_count):
        pairs = [(source, (source + step) % dp_count) for source in range(dp_count)]
        key_blocks.append(lax.ppermute(key_weight[0], "dp", pairs))
    by_step = jnp.stack(key_blocks, axis=0)
    source_step = (dp_index - jnp.arange(dp_count, dtype=jnp.int32)) % dp_count
    full_key = jnp.take(by_step, source_step, axis=0).reshape(model_width, model_width)
    last_phase = phase_count - 1
    head_pieces = []
    for source_phase in range(phase_count):
        if source_phase == last_phase:
            head_pieces.append(head_weight)
        else:
            head_pieces.append(lax.ppermute(head_weight, "pipe", [(source_phase, last_phase)]))
    head_full = jnp.concatenate(head_pieces, axis=1)
    section_gain = norm_gain[0]

    def attention(by_heads, frame_row):
        query_all = by_heads[0].reshape(seq_total, local_heads, HEAD)
        key_all = by_heads[1].reshape(seq_total, local_heads, HEAD)
        value_all = by_heads[2].reshape(seq_total, local_heads, HEAD)
        allowed = frame_row[None, :] <= frame_row[:, None]
        scores = (
            jnp.einsum("shd,khd->hsk", query_all, key_all, preferred_element_type=jnp.float32)
            * score_scale
        )
        scores = jnp.where(allowed[None], scores, -1e30)
        row_max = jnp.max(scores, axis=-1, keepdims=True)
        weights = jnp.where(allowed[None], jnp.exp(scores - row_max), 0.0)
        row_sum = jnp.sum(weights, axis=-1)
        mixed = jnp.einsum(
            "hsk,khd->hsd",
            weights.astype(jnp.bfloat16),
            value_all,
            preferred_element_type=jnp.float32,
        ) / row_sum[..., None]
        return mixed.transpose(1, 0, 2).reshape(seq_total, local_width).astype(jnp.bfloat16)

    incoming = jnp.zeros((1, local_rows, model_width), jnp.bfloat16)
    finals = []
    moment_count = micro_count + phase_count - 1
    for moment in range(moment_count):
        micro_slot = jnp.clip(moment - phase_index, 0, micro_count - 1)
        active = jnp.logical_and(moment >= phase_index, moment - phase_index < micro_count)
        current = jnp.where(phase_index == 0, embedded[min(moment, micro_count - 1)], incoming)
        frame_row = lax.dynamic_index_in_dim(frame_ids, micro_slot, 0, keepdims=False)[0]
        wide_state = current.astype(jnp.float32)
        normed = rms_scale(wide_state, section_gain).astype(jnp.bfloat16)[0]

        def project(source):
            queries = jnp.dot(source, full_query, preferred_element_type=jnp.float32).astype(
                jnp.bfloat16
            )
            if moment == 0:
                block_rows = model_width // dp_count
                by_block = source.reshape(local_rows, dp_count, block_rows)
                in_step_order = jnp.take(by_block, source_step, axis=1).reshape(
                    local_rows, model_width
                )
                step_key = by_step.reshape(model_width, model_width)
                keys = jnp.dot(in_step_order, step_key, preferred_element_type=jnp.float32)
            else:
                keys = jnp.dot(source, full_key, preferred_element_type=jnp.float32)
            keys = keys.astype(jnp.bfloat16)
            return jnp.stack((queries, keys, source), axis=0)

        def blank_triple(source):
            return jnp.zeros((3,) + source.shape, jnp.bfloat16)

        if moment == 0:
            value_heads = lax.all_to_all(
                normed[None], "ctx", split_axis=2, concat_axis=1, tiled=True
            )
            pair = lax.cond(active, project, blank_triple, normed)[:2]
            pair_heads = lax.all_to_all(pair, "ctx", split_axis=2, concat_axis=1, tiled=True)
            section_by_heads = jnp.concatenate((pair_heads, value_heads), axis=0)
        else:
            triple = lax.cond(active, project, blank_triple, normed)
            section_by_heads = lax.all_to_all(
                triple, "ctx", split_axis=2, concat_axis=1, tiled=True
            )

        def run_attention(arrived):
            return attention(arrived, frame_row)

        def blank_heads(arrived):
            return jnp.zeros((seq_total, local_width), jnp.bfloat16)

        mixed_heads = lax.cond(active, run_attention, blank_heads, section_by_heads)
        chunk = local_rows * local_width
        lanes = 128 if chunk % 128 == 0 else chunk
        outgoing = mixed_heads.reshape(cycle_size, chunk // lanes, lanes)
        returned = lax.all_to_all(outgoing, "ctx", split_axis=0, concat_axis=0, tiled=True)
        mixed = (
            returned.reshape(cycle_size, local_rows, local_width)
            .transpose(1, 0, 2)
            .reshape(local_rows, model_width)
        )
        result = (wide_state + mixed.astype(jnp.float32)[None]).astype(jnp.bfloat16)
        if moment + 1 < moment_count:
            incoming = shifted(result, "pipe", 1)
        if moment >= phase_count - 1:
            finals.append(result)
    final_state = jnp.stack(finals, axis=0)
    is_last = phase_index == last_phase
    head_cols = head_weight.shape[1]
    final_norm = rms_scale(final_state.astype(jnp.float32), head_gain).astype(jnp.bfloat16)
    velocity_all = jnp.einsum(
        "mbsd,dp->mbsp", final_norm, head_full, preferred_element_type=jnp.float32
    )
    residue = velocity_all - target
    grad_all = jnp.einsum(
        "mbsd,mbsp->dp", final_norm.astype(jnp.float32), residue, precision=lax.Precision.HIGHEST
    ) / float(seq_total)
    grad_rows = lax.psum_scatter(grad_all, "dp", scatter_dimension=0, tiled=True)
    grad_rows = lax.psum(grad_rows, "ctx")
    velocity_in = jnp.zeros(velocity_all.shape[:3] + (head_cols,), jnp.float32)
    gradient_in = jnp.zeros((grad_rows.shape[0], head_cols), jnp.float32)
    for target_phase in range(last_phase):
        cols = slice(target_phase * head_cols, (target_phase + 1) * head_cols)
        pair = [(last_phase, target_phase)]
        velocity_in = velocity_in + lax.ppermute(velocity_all[..., cols], "pipe", pair)
        gradient_in = gradient_in + lax.ppermute(grad_rows[:, cols], "pipe", pair)
    own_cols = slice(last_phase * head_cols, phase_count * head_cols)
    velocity = jnp.where(is_last, velocity_all[..., own_cols], velocity_in)
    gradient = jnp.where(is_last, grad_rows[:, own_cols], gradient_in)
    return (velocity, gradient)


def solution(mesh):
    placed = (
        P(None, "dp", "ctx", None),
        P(None, "dp", "ctx", None),
        P(None, "dp"),
        P(None, "dp", None),
        P(),
        P(),
        P("pipe", "dp", None),
        P("pipe", "dp", None),
        P("pipe", None),
        P(),
        P(None, "pipe"),
    )
    return jax.shard_map(
        on_device,
        mesh=mesh,
        in_specs=placed,
        out_specs=(P(None, "dp", "ctx", "pipe"), P("dp", "pipe")),
        check_vma=False,
    )
```

```python
import jax
import jax.numpy as jnp
from jax import lax
from jax.sharding import PartitionSpec as P

HEAD = 96


epsilon = 1e-06


def shifted(value, axis, steps):
    count = lax.axis_size(axis)
    first, last = (max(0, -steps), min(count, count - steps))
    return lax.ppermute(value, axis, [(source, source + steps) for source in range(first, last)])


def rms_scale(values, gain_row):
    return (
        values * lax.rsqrt(jnp.mean(values * values, axis=-1, keepdims=True) + epsilon) * gain_row
    )


def on_device(
    clean_latent,
    noise_latent,
    time_index,
    frame_ids,
    embed_weight,
    time_vector,
    query_weight,
    key_weight,
    norm_gain,
    head_gain,
    head_weight,
):
    phase_index = lax.axis_index("pipe")
    phase_count = lax.axis_size("pipe")
    cycle_size = lax.axis_size("ctx")
    micro_count = clean_latent.shape[0]
    local_rows = clean_latent.shape[2]
    model_width = embed_weight.shape[1]
    head_count = model_width // HEAD
    local_heads = head_count // cycle_size
    local_width = local_heads * HEAD
    seq_total = local_rows * cycle_size
    score_scale = HEAD ** (-0.5)
    flow_time = ((time_index.astype(jnp.float32) + 0.5) / 1000.0)[:, :, None, None]
    noisy_input = ((1.0 - flow_time) * noise_latent + flow_time * clean_latent).astype(jnp.bfloat16)
    target = clean_latent - noise_latent
    embedded = jnp.einsum(
        "mbsp,pd->mbsd", noisy_input, embed_weight, preferred_element_type=jnp.float32
    )
    embedded = (embedded + flow_time * time_vector).astype(jnp.bfloat16)
    dp_index = lax.axis_index("dp")
    dp_count = lax.axis_size("dp")
    full_query = lax.all_gather(query_weight[0], "dp", axis=0, tiled=True)
    key_blocks = [key_weight[0]]
    for step in range(1, dp_count):
        pairs = [(source, (source + step) % dp_count) for source in range(dp_count)]
        key_blocks.append(lax.ppermute(key_weight[0], "dp", pairs))
    by_step = jnp.stack(key_blocks, axis=0)
    source_step = (dp_index - jnp.arange(dp_count, dtype=jnp.int32)) % dp_count
    full_key = jnp.take(by_step, source_step, axis=0).reshape(model_width, model_width)
    last_phase = phase_count - 1
    head_pieces = []
    for source_phase in range(phase_count):
        if source_phase == last_phase:
            head_pieces.append(head_weight)
        else:
            head_pieces.append(lax.ppermute(head_weight, "pipe", [(source_phase, last_phase)]))
    head_full = jnp.concatenate(head_pieces, axis=1)
    section_gain = norm_gain[0]

    def attention(by_heads, frame_row):
        query_all = by_heads[0].reshape(seq_total, local_heads, HEAD)
        key_all = by_heads[1].reshape(seq_total, local_heads, HEAD)
        value_all = by_heads[2].reshape(seq_total, local_heads, HEAD)
        allowed = frame_row[None, :] <= frame_row[:, None]
        scores = (
            jnp.einsum("shd,khd->hsk", query_all, key_all, preferred_element_type=jnp.float32)
            * score_scale
        )
        scores = jnp.where(allowed[None], scores, -1e30)
        row_max = jnp.max(scores, axis=-1, keepdims=True)
        weights = jnp.where(allowed[None], jnp.exp(scores - row_max), 0.0)
        row_sum = jnp.sum(weights, axis=-1)
        mixed = jnp.einsum(
            "hsk,khd->hsd",
            weights.astype(jnp.bfloat16),
            value_all,
            preferred_element_type=jnp.float32,
        ) / row_sum[..., None]
        return mixed.transpose(1, 0, 2).reshape(seq_total, local_width).astype(jnp.bfloat16)

    incoming = jnp.zeros((1, local_rows, model_width), jnp.bfloat16)
    finals = []
    moment_count = micro_count + phase_count - 1
    for moment in range(moment_count):
        micro_slot = jnp.clip(moment - phase_index, 0, micro_count - 1)
        active = jnp.logical_and(moment >= phase_index, moment - phase_index < micro_count)
        current = jnp.where(phase_index == 0, embedded[min(moment, micro_count - 1)], incoming)
        frame_row = lax.dynamic_index_in_dim(frame_ids, micro_slot, 0, keepdims=False)[0]
        wide_state = current.astype(jnp.float32)
        normed = rms_scale(wide_state, section_gain).astype(jnp.bfloat16)[0]

        def project(source):
            queries = jnp.dot(source, full_query, preferred_element_type=jnp.float32).astype(
                jnp.bfloat16
            )
            keys = jnp.dot(source, full_key, preferred_element_type=jnp.float32).astype(
                jnp.bfloat16
            )
            return jnp.stack((queries, keys, source), axis=0)

        def blank_triple(source):
            return jnp.zeros((3,) + source.shape, jnp.bfloat16)

        if moment == 0:
            value_heads = lax.all_to_all(
                normed[None], "ctx", split_axis=2, concat_axis=1, tiled=True
            )
            def project_one(source, weight):
                return jnp.dot(source, weight, preferred_element_type=jnp.float32).astype(
                    jnp.bfloat16
                )[None]

            def blank_one(source, weight):
                return jnp.zeros((1,) + source.shape, jnp.bfloat16)

            query_rows = lax.cond(active, project_one, blank_one, normed, full_query)
            query_heads = lax.all_to_all(
                query_rows, "ctx", split_axis=2, concat_axis=1, tiled=True
            )
            key_rows = lax.cond(active, project_one, blank_one, normed, full_key)
            key_heads = lax.all_to_all(key_rows, "ctx", split_axis=2, concat_axis=1, tiled=True)
            section_by_heads = jnp.concatenate((query_heads, key_heads, value_heads), axis=0)
        else:
            triple = lax.cond(active, project, blank_triple, normed)
            section_by_heads = lax.all_to_all(
                triple, "ctx", split_axis=2, concat_axis=1, tiled=True
            )

        def run_attention(arrived):
            return attention(arrived, frame_row)

        def blank_heads(arrived):
            return jnp.zeros((seq_total, local_width), jnp.bfloat16)

        mixed_heads = lax.cond(active, run_attention, blank_heads, section_by_heads)
        chunk = local_rows * local_width
        lanes = 128 if chunk % 128 == 0 else chunk
        outgoing = mixed_heads.reshape(cycle_size, chunk // lanes, lanes)
        returned = lax.all_to_all(outgoing, "ctx", split_axis=0, concat_axis=0, tiled=True)
        mixed = (
            returned.reshape(cycle_size, local_rows, local_width)
            .transpose(1, 0, 2)
            .reshape(local_rows, model_width)
        )
        result = (wide_state + mixed.astype(jnp.float32)[None]).astype(jnp.bfloat16)
        if moment + 1 < moment_count:
            incoming = shifted(result, "pipe", 1)
        if moment >= phase_count - 1:
            finals.append(result)
    final_state = jnp.stack(finals, axis=0)
    is_last = phase_index == last_phase
    head_cols = head_weight.shape[1]
    final_norm = rms_scale(final_state.astype(jnp.float32), head_gain).astype(jnp.bfloat16)
    velocity_all = jnp.einsum(
        "mbsd,dp->mbsp", final_norm, head_full, preferred_element_type=jnp.float32
    )
    residue = velocity_all - target
    grad_all = jnp.einsum(
        "mbsd,mbsp->dp", final_norm.astype(jnp.float32), residue, precision=lax.Precision.HIGHEST
    ) / float(seq_total)
    grad_rows = lax.psum_scatter(grad_all, "dp", scatter_dimension=0, tiled=True)
    grad_rows = lax.psum(grad_rows, "ctx")
    velocity_in = jnp.zeros(velocity_all.shape[:3] + (head_cols,), jnp.float32)
    gradient_in = jnp.zeros((grad_rows.shape[0], head_cols), jnp.float32)
    for target_phase in range(last_phase):
        cols = slice(target_phase * head_cols, (target_phase + 1) * head_cols)
        pair = [(last_phase, target_phase)]
        velocity_in = velocity_in + lax.ppermute(velocity_all[..., cols], "pipe", pair)
        gradient_in = gradient_in + lax.ppermute(grad_rows[:, cols], "pipe", pair)
    own_cols = slice(last_phase * head_cols, phase_count * head_cols)
    velocity = jnp.where(is_last, velocity_all[..., own_cols], velocity_in)
    gradient = jnp.where(is_last, grad_rows[:, own_cols], gradient_in)
    return (velocity, gradient)


def solution(mesh):
    placed = (
        P(None, "dp", "ctx", None),
        P(None, "dp", "ctx", None),
        P(None, "dp"),
        P(None, "dp", None),
        P(),
        P(),
        P("pipe", "dp", None),
        P("pipe", "dp", None),
        P("pipe", None),
        P(),
        P(None, "pipe"),
    )
    return jax.shard_map(
        on_device,
        mesh=mesh,
        in_specs=placed,
        out_specs=(P(None, "dp", "ctx", "pipe"), P("dp", "pipe")),
        check_vma=False,
    )
```
